128 devices in a mesh: row: 8 (over y, core), col: 16 (over x, z).
Axes of the slice: x: 4, y: 4, z: 4, core: 2. Of those that a mesh axis runs over, the one named last changes fastest.
Arguments:
- occ_coeffs: bfloat16 [49152, 20480], P('row', 'col'), may hold values from -0.21875 to 0.21875
- colloc: bfloat16 [1024, 1024, 512], P(('row', 'col')), may hold values from -6 to 6
- grid_points: float32 [1024, 3, 512], P(('row', 'col')), may hold values from -4 to 4
- grid_weights: float32 [1024, 512], P(('row', 'col')), may hold values from 0.01 to 0.1
- charge_sites: float32 [3, 512], replicated, may hold values from -4 to 4
- charge_proj: bfloat16 [512, 128], replicated, may hold values from -0.5 to 0.5
- shell_lists: int32 [1024, 16], P(('row', 'col')), may hold values from 0 to 767, as said below
- point_counts: int32 [1024], P(('row', 'col')), may hold values from 1 to 512, as said below
Outputs:
- exchange_slab: float32 [49152, 128], P(('row', 'col'))
The draws below stay inside these ranges and needn't reach their ends.
Inputs may be any that keep to these rules, and one draw needn't show every extreme that they name: `shell_lists`: batches b * 8 to b * 8 + 7 belong to the b-th device in row+col order, and the blocks named by one device's batches are all different. Owner device o holds blocks o * 6 to o * 6 + 5; one device's batches name at most 2 blocks of one owner, and in every draw one owner gets exactly 2 from every device. `point_counts`: points of a batch beyond its count are not part of it.
All inputs are finite; a program needn't handle non-finite values.
Results may differ from the reference program's by a relative error of at most 0.0045.
Values may be sent and summed in bfloat16 or wider, within the bound.
No kernel may reach another device: no remote copies, remote signals or barrier semaphores. Data moves between devices by JAX's collectives and lax.ppermute only.
A program may use at most 128 MiB of HBM per device.

```python
import math
import jax
import jax.numpy as jnp
from jax import lax

NBF = 49152
NOCC = 20480
SH = 64
NSIG = 16
SLAB = 128
BATCH_DEV = 8
PTS = 512
NAUX = 512
BATCHES = 1024
OWN_BLOCKS = 6
CAP = 2
N_ROW = 8
N_COL = 16


def draw_shell_lists(key, part):
    owners = N_ROW * N_COL
    half = CAP // 2
    common_owner = jax.random.randint(jax.random.fold_in(key, 7), (), 0, owners)

    def one_device(device):
        device_key = jax.random.fold_in(jax.random.fold_in(key, 11), device)
        key_order, key_shift, key_offset, key_place = jax.random.split(device_key, 4)
        order = jax.random.permutation(key_order, owners)
        order = (order - order[0] + common_owner) % owners
        shifts = jax.random.randint(key_shift, (owners // 2,), -half, half + 1)
        shifts = shifts.at[0].set(half)
        counts = jnp.zeros((owners,), jnp.int32)
        counts = counts.at[order[0::2]].set(half + shifts)
        counts = counts.at[order[1::2]].set(half - shifts)
        offsets = jax.random.randint(key_offset, (owners,), 0, OWN_BLOCKS)
        places = jnp.arange(CAP)
        table = jnp.arange(owners)[:, None] * OWN_BLOCKS + (places[None, :] + offsets[:, None]) % OWN_BLOCKS
        valid = places[None, :] < counts[:, None]
        ranking = jnp.argsort(jnp.where(valid, 0, 1).reshape(-1), stable=True)
        picked = table.reshape(-1)[ranking[:BATCH_DEV * NSIG]]
        picked = jax.random.permutation(key_place, picked)
        return jnp.sort(picked.reshape(BATCH_DEV, NSIG), axis=1)
    lists = jax.vmap(one_device)(jnp.arange(owners))
    return lists.reshape(BATCHES, NSIG).astype(jnp.int32)


def draw_point_counts(key, part):
    owners = N_ROW * N_COL
    key_level, key_raw, key_pick = jax.random.split(jax.random.fold_in(key, 23), 3)
    levels = jax.random.randint(key_level, (owners, 1), 1, 5)
    tops = jnp.maximum(levels * PTS // 4, 1)
    raw = jax.random.randint(key_raw, (owners, BATCH_DEV), 0, PTS)
    counts = (1 + raw % tops).reshape(-1)
    chosen = jax.random.randint(key_pick, (), 0, BATCHES)
    counts = counts.at[chosen].set(PTS)
    return counts.astype(jnp.int32)


def steps_of(stream_key, extent, shards, smallest, high):
    def one(dim, blocks):
        draws = jax.random.uniform(jax.random.fold_in(jax.random.fold_in(stream_key, 6), dim), (blocks,), jnp.float32, smallest / len(shards), high / len(shards))
        return jnp.repeat(jnp.exp(draws), extent[dim] // blocks).reshape((-1,) + (1,) * (len(extent) - dim - 1))

    factor_of = one(*shards[0])
    for cut in shards[1:]:
        factor_of = factor_of * one(*cut)
    return factor_of


def noise(stream_key, extent, spread, limit, cuts=(), held_as=jnp.bfloat16):
    array = jax.random.normal(stream_key, extent, jnp.float32) * spread
    if len(cuts) > 0:
        array = steps_of(stream_key, extent, cuts, -0.22, 0.18) * array
    return jnp.clip(array, min=-limit, max=limit).astype(held_as)


def setup_inputs(seed: int = 0) -> dict:
    keys = jax.random.split(jax.random.key(seed), 9)
    occ_coeffs = noise(keys[0], (NBF, NOCC), ((NOCC * NSIG * SH) ** -0.25), 0.21875, ((0, 8), (1, 16)))
    colloc = noise(keys[1], (BATCHES, NSIG * SH, PTS), 1.0, 6.0, ((0, 128),))
    grid_points = jnp.clip(jax.random.uniform(keys[2], (BATCHES, 3, PTS), jnp.float32, -4.0, 4.0) * steps_of(keys[2], (BATCHES, 3, PTS), ((0, 128),), -0.4, 0.0), -4.0, 4.0)
    grid_weights = jnp.clip(jnp.exp(math.log(0.1) - 2.3025851 * jax.random.uniform(keys[3], (BATCHES, PTS), jnp.float32) ** steps_of(keys[3], (BATCHES, PTS), ((0, 128),), -0.2, 0.2)), 0.01, 0.1)
    charge_sites = jnp.clip(jax.random.uniform(keys[4], (3, NAUX), jnp.float32, -4.0, 4.0), -4.0, 4.0)
    charge_proj = noise(keys[5], (NAUX, SLAB), SLAB ** -0.5, 0.5)
    shell_lists = draw_shell_lists(jax.random.fold_in(keys[8], 71), 0)
    point_counts = draw_point_counts(jax.random.fold_in(keys[8], 71), 0)
    return dict(occ_coeffs=occ_coeffs, colloc=colloc, grid_points=grid_points, grid_weights=grid_weights, charge_sites=charge_sites, charge_proj=charge_proj, shell_lists=shell_lists, point_counts=point_counts)


smear_sq = 0.25

def potential(points, charge_sites):
    dist_sq = (points[0][None, :] - charge_sites[0][:, None]) ** 2
    dist_sq = dist_sq + (points[1][None, :] - charge_sites[1][:, None]) ** 2
    dist_sq = dist_sq + (points[2][None, :] - charge_sites[2][:, None]) ** 2
    return lax.rsqrt(dist_sq + smear_sq)

def reference(occ_coeffs, colloc, grid_points, grid_weights, charge_sites, charge_proj, shell_lists, point_counts):
    density = jnp.dot(occ_coeffs, occ_coeffs[:SLAB].T, preferred_element_type=jnp.float32).astype(jnp.bfloat16)
    blocks = density.reshape(NBF // SH, SH, SLAB)

    def one_batch(carry, item):
        block_ids, batch_colloc, batch_points, batch_weights, count = item
        fetched = blocks[block_ids].reshape(NSIG * SH, SLAB)
        field = lax.dot_general(fetched, batch_colloc, (((0,), (0,)), ((), ())), preferred_element_type=jnp.float32).astype(jnp.bfloat16)
        projected = jnp.dot(charge_proj, field, preferred_element_type=jnp.float32)
        live = (jnp.arange(PTS) < count).astype(jnp.float32)
        charges = (projected * potential(batch_points, charge_sites) * (batch_weights * live)[None, :]).astype(jnp.bfloat16)
        spread_back = lax.dot_general(charge_proj, charges, (((0,), (0,)), ((), ())), preferred_element_type=jnp.float32).astype(jnp.bfloat16)
        term = lax.dot_general(batch_colloc, spread_back, (((1,), (1,)), ((), ())), preferred_element_type=jnp.float32)
        carry = carry.at[block_ids].add(term.reshape(NSIG, SH * SLAB))
        return (carry, None)
    start_value = jnp.zeros((NBF // SH, SH * SLAB), jnp.float32)
    summed, _ = lax.scan(one_batch, start_value, (shell_lists, colloc, grid_points, grid_weights, point_counts))
    return summed.reshape(NBF, SLAB)
```

```python
import jax
import jax.numpy as jnp
from jax import lax
from jax.sharding import PartitionSpec as P

SH = 64
NSIG = 16


smear_sq = 0.25


def broadcast_from_first(value, axis):
    size = lax.axis_size(axis)
    index = lax.axis_index(axis)
    have = 1
    while have < size:
        pairs = [(src, src + have) for src in range(have) if src + have < size]
        moved = lax.ppermute(value, axis, pairs)
        value = jnp.where(index >= have, moved, value)
        have *= 2
    return value


def potential(points, charge_sites):
    dist_sq = (points[:, 0][:, None, :] - charge_sites[0][None, :, None]) ** 2
    dist_sq = dist_sq + (points[:, 1][:, None, :] - charge_sites[1][None, :, None]) ** 2
    dist_sq = dist_sq + (points[:, 2][:, None, :] - charge_sites[2][None, :, None]) ** 2
    return lax.rsqrt(dist_sq + smear_sq)


def batch_terms(dens_rows, colloc, grid_points, grid_weights, charge_sites, charge_proj, point_counts):
    total_points = colloc.shape[2]
    field = jnp.einsum(
        "bfs,bfp->bsp", dens_rows, colloc, preferred_element_type=jnp.float32
    ).astype(jnp.bfloat16)
    projected = jnp.einsum("ks,bsp->bkp", charge_proj, field, preferred_element_type=jnp.float32)
    live = (jnp.arange(total_points)[None, :] < point_counts[:, None]).astype(jnp.float32)
    charges = (
        projected * potential(grid_points, charge_sites) * (grid_weights * live)[:, None, :]
    ).astype(jnp.bfloat16)
    spread_back = jnp.einsum(
        "ks,bkp->bsp", charge_proj, charges, preferred_element_type=jnp.float32
    ).astype(jnp.bfloat16)
    return jnp.einsum("bfp,bsp->bfs", colloc, spread_back, preferred_element_type=jnp.float32)


def on_device(
    occ_coeffs,
    colloc,
    grid_points,
    grid_weights,
    charge_sites,
    charge_proj,
    shell_lists,
    point_counts,
):
    row_count = lax.axis_size("row")
    col_count = lax.axis_size("col")
    owners = row_count * col_count
    me = lax.axis_index("row") * col_count + lax.axis_index("col")
    group_rows = occ_coeffs.shape[0]
    slab_width = charge_proj.shape[1]
    own_rows = group_rows // col_count
    own_blocks = own_rows // SH
    tile = SH * slab_width

    all_lists = lax.all_gather(shell_lists, ("row", "col"), tiled=True)
    window = broadcast_from_first(occ_coeffs[:slab_width], "row")

    requested = shell_lists.reshape(-1)
    request_count = requested.shape[0]
    capacity = 2 * request_count // owners
    slots = owners * capacity
    owner = requested // own_blocks
    onehot = (owner[:, None] == jnp.arange(owners)[None, :]).astype(jnp.int32)
    before = jnp.cumsum(onehot, axis=0) - onehot
    rank = jnp.sum(before * onehot, axis=1)
    slot = owner * capacity + rank
    pick = (slot[:, None] == jnp.arange(slots)[None, :]).astype(jnp.bfloat16)

    lists = all_lists.reshape(owners, request_count)
    mine = (lists // own_blocks == me).astype(jnp.int32)
    order = jnp.cumsum(mine, axis=1)
    local = lists % own_blocks
    wanted_by = []
    for place in range(capacity):
        hit = mine * (order == place + 1)
        wanted_by.append(
            jnp.sum(hit * (local + 1), axis=1) - 1
        )
    received_ids = jnp.stack(wanted_by, axis=1).reshape(-1)
    serve = (received_ids[:, None] == jnp.arange(own_blocks)[None, :]).astype(jnp.bfloat16)

    density = lax.psum_scatter(
        lax.dot_general(
            occ_coeffs, window, (((1,), (1,)), ((), ())), preferred_element_type=jnp.float32
        ),
        "col",
        scatter_dimension=0,
        tiled=True,
    ).astype(jnp.bfloat16)
    store = density.reshape(own_blocks, tile)
    found = jnp.dot(serve, store, preferred_element_type=jnp.float32).astype(jnp.bfloat16)
    replies = lax.all_to_all(
        found.reshape(owners, capacity, tile), ("row", "col"), split_axis=0, concat_axis=0, tiled=True
    )
    fetched = jnp.dot(
        pick, replies.reshape(slots, tile), preferred_element_type=jnp.float32
    ).astype(jnp.bfloat16)
    dens_rows = fetched.reshape(shell_lists.shape[0], NSIG * SH, slab_width)
    terms = batch_terms(
        dens_rows, colloc, grid_points, grid_weights, charge_sites, charge_proj, point_counts
    )
    terms = terms.astype(jnp.bfloat16).reshape(request_count, tile)
    tiles = lax.dot_general(
        pick, terms, (((0,), (0,)), ((), ())), preferred_element_type=jnp.float32
    ).astype(jnp.bfloat16)
    arrived = lax.all_to_all(
        tiles.reshape(owners, capacity, tile), ("row", "col"), split_axis=0, concat_axis=0, tiled=True
    )
    summed = lax.dot_general(
        serve, arrived.reshape(slots, tile), (((0,), (0,)), ((), ())), preferred_element_type=jnp.float32
    )
    return summed.reshape(own_rows, slab_width)


def solution(mesh):
    placed = (
        P("row", "col"),
        P(("row", "col"), None, None),
        P(("row", "col"), None, None),
        P(("row", "col"), None),
        P(),
        P(),
        P(("row", "col"), None),
        P(("row", "col")),
    )
    return jax.shard_map(
        on_device, mesh=mesh, in_specs=placed, out_specs=P(("row", "col"), None), check_vma=False
    )
```

```python
import jax
import jax.numpy as jnp
from jax import lax
from jax.sharding import PartitionSpec as P

SH = 64
NSIG = 16


smear_sq = 0.25


def broadcast_from_first(value, axis):
    size = lax.axis_size(axis)
    index = lax.axis_index(axis)
    have = 1
    while have < size:
        pairs = [(src, src + have) for src in range(have) if src + have < size]
        moved = lax.ppermute(value, axis, pairs)
        value = jnp.where(index >= have, moved, value)
        have *= 2
    return value


def potential(points, charge_sites):
    dist_sq = (points[:, 0][:, None, :] - charge_sites[0][None, :, None]) ** 2
    dist_sq = dist_sq + (points[:, 1][:, None, :] - charge_sites[1][None, :, None]) ** 2
    dist_sq = dist_sq + (points[:, 2][:, None, :] - charge_sites[2][None, :, None]) ** 2
    return lax.rsqrt(dist_sq + smear_sq)


def batch_terms(dens_rows, colloc, grid_points, grid_weights, charge_sites, charge_proj, point_counts):
    total_points = colloc.shape[2]
    field = jnp.einsum(
        "bfs,bfp->bsp", dens_rows, colloc, preferred_element_type=jnp.float32
    ).astype(jnp.bfloat16)
    projected = jnp.einsum("ks,bsp->bkp", charge_proj, field, preferred_element_type=jnp.float32)
    live = (jnp.arange(total_points)[None, :] < point_counts[:, None]).astype(jnp.float32)
    charges = (
        projected * potential(grid_points, charge_sites) * (grid_weights * live)[:, None, :]
    ).astype(jnp.bfloat16)
    spread_back = jnp.einsum(
        "ks,bkp->bsp", charge_proj, charges, preferred_element_type=jnp.float32
    ).astype(jnp.bfloat16)
    return jnp.einsum("bfp,bsp->bfs", colloc, spread_back, preferred_element_type=jnp.float32)


def on_device(
    occ_coeffs,
    colloc,
    grid_points,
    grid_weights,
    charge_sites,
    charge_proj,
    shell_lists,
    point_counts,
):
    row_count = lax.axis_size("row")
    col_count = lax.axis_size("col")
    owners = row_count * col_count
    me = lax.axis_index("row") * col_count + lax.axis_index("col")
    group_rows = occ_coeffs.shape[0]
    slab_width = charge_proj.shape[1]
    own_rows = group_rows // col_count
    own_blocks = own_rows // SH

    window = broadcast_from_first(occ_coeffs[:slab_width], "row")

    requested = shell_lists.reshape(-1)
    request_count = requested.shape[0]
    capacity = 2 * request_count // owners
    slots = owners * capacity
    owner = requested // own_blocks
    onehot = (owner[:, None] == jnp.arange(owners)[None, :]).astype(jnp.int32)
    before = jnp.cumsum(onehot, axis=0) - onehot
    rank = jnp.sum(before * onehot, axis=1)
    slot = owner * capacity + rank
    hit = slot[None, :] == jnp.arange(slots)[:, None]
    source_of = jnp.sum(
        jnp.where(hit, jnp.arange(request_count)[None, :] - request_count, 0), axis=1
    ) + request_count
    wanted = jnp.full((slots,), -1, jnp.int32).at[slot].set(requested % own_blocks)
    received_ids = lax.all_to_all(
        wanted.reshape(owners, capacity), ("row", "col"), split_axis=0, concat_axis=0, tiled=True
    ).reshape(-1)

    density = lax.psum_scatter(
        lax.dot_general(
            occ_coeffs, window, (((1,), (1,)), ((), ())), preferred_element_type=jnp.float32
        ),
        "col",
        scatter_dimension=0,
        tiled=True,
    ).astype(jnp.bfloat16)
    store = density.reshape(own_blocks, SH, slab_width)
    found = store[jnp.maximum(received_ids, 0)]
    replies = lax.all_to_all(
        found.reshape(owners, capacity * SH, slab_width),
        ("row", "col"),
        split_axis=0,
        concat_axis=0,
        tiled=True,
    )
    fetched = replies.reshape(slots, SH, slab_width)[slot]
    dens_rows = fetched.reshape(shell_lists.shape[0], NSIG * SH, slab_width)
    terms = batch_terms(
        dens_rows, colloc, grid_points, grid_weights, charge_sites, charge_proj, point_counts
    )
    terms = terms.astype(jnp.bfloat16).reshape(request_count, SH, slab_width)
    tiles = jnp.take(terms, source_of, axis=0, mode="fill", fill_value=0)
    arrived = lax.all_to_all(
        tiles.reshape(owners, capacity * SH, slab_width),
        ("row", "col"),
        split_axis=0,
        concat_axis=0,
        tiled=True,
    )
    serve = (jnp.arange(own_blocks)[:, None] == received_ids[None, :]).astype(jnp.bfloat16)
    summed = jnp.einsum(
        "js,sfc->jfc", serve, arrived.reshape(slots, SH, slab_width), preferred_element_type=jnp.float32
    )
    return summed.reshape(own_rows, slab_width)


def solution(mesh):
    placed = (
        P("row", "col"),
        P(("row", "col"), None, None),
        P(("row", "col"), None, None),
        P(("row", "col"), None),
        P(),
        P(),
        P(("row", "col"), None),
        P(("row", "col")),
    )
    return jax.shard_map(
        on_device, mesh=mesh, in_specs=placed, out_specs=P(("row", "col"), None), check_vma=False
    )
```

```python
import jax
import jax.numpy as jnp
from jax import lax
from jax.sharding import PartitionSpec as P

SH = 64
NSIG = 16


smear_sq = 0.25


def broadcast_from_first(value, axis):
    size = lax.axis_size(axis)
    index = lax.axis_index(axis)
    have = 1
    while have < size:
        pairs = [(src, src + have) for src in range(have) if src + have < size]
        moved = lax.ppermute(value, axis, pairs)
        value = jnp.where(index >= have, moved, value)
        have *= 2
    return value


def potential(points, charge_sites):
    dist_sq = (points[:, 0][:, None, :] - charge_sites[0][None, :, None]) ** 2
    dist_sq = dist_sq + (points[:, 1][:, None, :] - charge_sites[1][None, :, None]) ** 2
    dist_sq = dist_sq + (points[:, 2][:, None, :] - charge_sites[2][None, :, None]) ** 2
    return lax.rsqrt(dist_sq + smear_sq)


def batch_terms(dens_rows, colloc, grid_points, grid_weights, charge_sites, charge_proj, point_counts):
    total_points = colloc.shape[2]
    field = jnp.einsum(
        "bfs,bfp->bsp", dens_rows, colloc, preferred_element_type=jnp.float32
    ).astype(jnp.bfloat16)
    projected = jnp.einsum("ks,bsp->bkp", charge_proj, field, preferred_element_type=jnp.float32)
    live = (jnp.arange(total_points)[None, :] < point_counts[:, None]).astype(jnp.float32)
    charges = (
        projected * potential(grid_points, charge_sites) * (grid_weights * live)[:, None, :]
    ).astype(jnp.bfloat16)
    spread_back = jnp.einsum(
        "ks,bkp->bsp", charge_proj, charges, preferred_element_type=jnp.float32
    ).astype(jnp.bfloat16)
    return jnp.einsum("bfp,bsp->bfs", colloc, spread_back, preferred_element_type=jnp.float32)


def on_device(
    occ_coeffs,
    colloc,
    grid_points,
    grid_weights,
    charge_sites,
    charge_proj,
    shell_lists,
    point_counts,
):
    row_count = lax.axis_size("row")
    col_count = lax.axis_size("col")
    owners = row_count * col_count
    me = lax.axis_index("row") * col_count + lax.axis_index("col")
    group_rows = occ_coeffs.shape[0]
    slab_width = charge_proj.shape[1]
    own_rows = group_rows // col_count
    own_blocks = own_rows // SH

    window = broadcast_from_first(occ_coeffs[:slab_width], "row")

    requested = shell_lists.reshape(-1)
    request_count = requested.shape[0]
    capacity = 2 * request_count // owners
    slots = owners * capacity
    owner = requested // own_blocks
    onehot = (owner[:, None] == jnp.arange(owners)[None, :]).astype(jnp.int32)
    before = jnp.cumsum(onehot, axis=0) - onehot
    rank = jnp.sum(before * onehot, axis=1)
    slot = owner * capacity + rank
    hit = slot[None, :] == jnp.arange(slots)[:, None]
    source_of = jnp.sum(
        jnp.where(hit, jnp.arange(request_count)[None, :] - request_count, 0), axis=1
    ) + request_count
    wanted = jnp.full((slots,), -1, jnp.int32).at[slot].set(requested % own_blocks)
    received_ids = lax.all_to_all(
        wanted.reshape(owners, capacity), ("row", "col"), split_axis=0, concat_axis=0, tiled=True
    ).reshape(-1)

    partial = lax.dot_general(
        occ_coeffs, window, (((1,), (1,)), ((), ())), preferred_element_type=jnp.float32
    )
    pieces = lax.all_to_all(
        partial.reshape(col_count, own_rows, slab_width), "col", split_axis=0, concat_axis=0, tiled=True
    )
    density = jnp.sum(pieces, axis=0).astype(jnp.bfloat16)
    store = density.reshape(own_blocks, SH, slab_width)
    found = store[jnp.maximum(received_ids, 0)]
    replies = lax.all_to_all(
        found.reshape(owners, capacity * SH, slab_width),
        ("row", "col"),
        split_axis=0,
        concat_axis=0,
        tiled=True,
    )
    fetched = replies.reshape(slots, SH, slab_width)[slot]
    dens_rows = fetched.reshape(shell_lists.shape[0], NSIG * SH, slab_width)
    terms = batch_terms(
        dens_rows, colloc, grid_points, grid_weights, charge_sites, charge_proj, point_counts
    )
    terms = terms.astype(jnp.bfloat16).reshape(request_count, SH, slab_width)
    tiles = jnp.take(terms, source_of, axis=0, mode="fill", fill_value=0)
    arrived = lax.all_to_all(
        tiles.reshape(owners, capacity * SH, slab_width),
        ("row", "col"),
        split_axis=0,
        concat_axis=0,
        tiled=True,
    )
    serve = (jnp.arange(own_blocks)[:, None] == received_ids[None, :]).astype(jnp.bfloat16)
    summed = jnp.einsum(
        "js,sfc->jfc", serve, arrived.reshape(slots, SH, slab_width), preferred_element_type=jnp.float32
    )
    return summed.reshape(own_rows, slab_width)


def solution(mesh):
    placed = (
        P("row", "col"),
        P(("row", "col"), None, None),
        P(("row", "col"), None, None),
        P(("row", "col"), None),
        P(),
        P(),
        P(("row", "col"), None),
        P(("row", "col")),
    )
    return jax.shard_map(
        on_device, mesh=mesh, in_specs=placed, out_specs=P(("row", "col"), None), check_vma=False
    )
```

```python
import jax
import jax.numpy as jnp
from jax import lax
from jax.sharding import PartitionSpec as P

SH = 64
NSIG = 16


smear_sq = 0.25


def broadcast_from_first(value, axis):
    size = lax.axis_size(axis)
    index = lax.axis_index(axis)
    have = 1
    while have < size:
        pairs = [(src, src + have) for src in range(have) if src + have < size]
        moved = lax.ppermute(value, axis, pairs)
        value = jnp.where(index >= have, moved, value)
        have *= 2
    return value


def potential(points, charge_sites):
    dist_sq = (points[:, 0][:, None, :] - charge_sites[0][None, :, None]) ** 2
    dist_sq = dist_sq + (points[:, 1][:, None, :] - charge_sites[1][None, :, None]) ** 2
    dist_sq = dist_sq + (points[:, 2][:, None, :] - charge_sites[2][None, :, None]) ** 2
    return lax.rsqrt(dist_sq + smear_sq)


def batch_terms(dens_rows, colloc, grid_points, grid_weights, charge_sites, charge_proj, point_counts):
    total_points = colloc.shape[2]
    field = jnp.einsum(
        "bfs,bfp->bsp", dens_rows, colloc, preferred_element_type=jnp.float32
    ).astype(jnp.bfloat16)
    projected = jnp.einsum("ks,bsp->bkp", charge_proj, field, preferred_element_type=jnp.float32)
    live = (jnp.arange(total_points)[None, :] < point_counts[:, None]).astype(jnp.float32)
    charges = (
        projected * potential(grid_points, charge_sites) * (grid_weights * live)[:, None, :]
    ).astype(jnp.bfloat16)
    spread_back = jnp.einsum(
        "ks,bkp->bsp", charge_proj, charges, preferred_element_type=jnp.float32
    ).astype(jnp.bfloat16)
    return jnp.einsum("bfp,bsp->bfs", colloc, spread_back, preferred_element_type=jnp.float32)


def on_device(
    occ_coeffs,
    colloc,
    grid_points,
    grid_weights,
    charge_sites,
    charge_proj,
    shell_lists,
    point_counts,
):
    row_count = lax.axis_size("row")
    col_count = lax.axis_size("col")
    owners = row_count * col_count
    me = lax.axis_index("row") * col_count + lax.axis_index("col")
    group_rows = occ_coeffs.shape[0]
    slab_width = charge_proj.shape[1]
    own_rows = group_rows // col_count
    own_blocks = own_rows // SH

    window = broadcast_from_first(occ_coeffs[:slab_width], "row")

    requested = shell_lists.reshape(-1)
    request_count = requested.shape[0]
    capacity = 2 * request_count // owners
    slots = owners * capacity
    owner = requested // own_blocks
    onehot = (owner[:, None] == jnp.arange(owners)[None, :]).astype(jnp.int32)
    before = jnp.cumsum(onehot, axis=0) - onehot
    rank = jnp.sum(before * onehot, axis=1)
    slot = owner * capacity + rank
    hit = slot[None, :] == jnp.arange(slots)[:, None]
    source_of = jnp.sum(jnp.where(hit, jnp.arange(request_count)[None, :], 0), axis=1)
    wanted = jnp.full((slots,), -1, jnp.int32).at[slot].set(requested % own_blocks)
    received_ids = lax.all_to_all(
        wanted.reshape(owners, capacity), ("row", "col"), split_axis=0, concat_axis=0, tiled=True
    ).reshape(-1)

    partial = lax.dot_general(
        occ_coeffs, window, (((1,), (1,)), ((), ())), preferred_element_type=jnp.float32
    )
    pieces = lax.all_to_all(
        partial.astype(jnp.bfloat16).reshape(col_count, own_rows, slab_width),
        "col",
        split_axis=0,
        concat_axis=0,
        tiled=True,
    )
    density = jnp.sum(pieces.astype(jnp.float32), axis=0).astype(jnp.bfloat16)
    store = density.reshape(own_blocks, SH, slab_width)
    found = store[jnp.maximum(received_ids, 0)]
    replies = lax.all_to_all(
        found.reshape(owners, capacity * SH, slab_width),
        ("row", "col"),
        split_axis=0,
        concat_axis=0,
        tiled=True,
    )
    fetched = replies.reshape(slots, SH, slab_width)[slot]
    dens_rows = fetched.reshape(shell_lists.shape[0], NSIG * SH, slab_width)
    terms = batch_terms(
        dens_rows, colloc, grid_points, grid_weights, charge_sites, charge_proj, point_counts
    )
    terms = terms.astype(jnp.bfloat16).reshape(request_count, SH, slab_width)
    tiles = terms[source_of]
    arrived = lax.all_to_all(
        tiles.reshape(owners, capacity * SH, slab_width),
        ("row", "col"),
        split_axis=0,
        concat_axis=0,
        tiled=True,
    )
    serve = (jnp.arange(own_blocks)[:, None] == received_ids[None, :]).astype(jnp.bfloat16)
    summed = jnp.einsum(
        "js,sfc->jfc", serve, arrived.reshape(slots, SH, slab_width), preferred_element_type=jnp.float32
    )
    return summed.reshape(own_rows, slab_width)


def solution(mesh):
    placed = (
        P("row", "col"),
        P(("row", "col"), None, None),
        P(("row", "col"), None, None),
        P(("row", "col"), None),
        P(),
        P(),
        P(("row", "col"), None),
        P(("row", "col")),
    )
    return jax.shard_map(
        on_device, mesh=mesh, in_specs=placed, out_specs=P(("row", "col"), None), check_vma=False
    )
```

```python
import jax
import jax.numpy as jnp
from jax import lax
from jax.sharding import PartitionSpec as P

SH = 64
NSIG = 16


smear_sq = 0.25


def broadcast_from_first(value, axis):
    size = lax.axis_size(axis)
    index = lax.axis_index(axis)
    have = 1
    while have < size:
        pairs = [(src, src + have) for src in range(have) if src + have < size]
        moved = lax.ppermute(value, axis, pairs)
        value = jnp.where(index >= have, moved, value)
        have *= 2
    return value


def potential(points, charge_sites):
    dist_sq = (points[:, 0][:, None, :] - charge_sites[0][None, :, None]) ** 2
    dist_sq = dist_sq + (points[:, 1][:, None, :] - charge_sites[1][None, :, None]) ** 2
    dist_sq = dist_sq + (points[:, 2][:, None, :] - charge_sites[2][None, :, None]) ** 2
    return lax.rsqrt(dist_sq + smear_sq)


def batch_terms(dens_rows, colloc, grid_points, grid_weights, charge_sites, charge_proj, point_counts):
    total_points = colloc.shape[2]
    field = jnp.einsum(
        "bfs,bfp->bsp", dens_rows, colloc, preferred_element_type=jnp.float32
    ).astype(jnp.bfloat16)
    projected = jnp.einsum("ks,bsp->bkp", charge_proj, field, preferred_element_type=jnp.float32)
    live = (jnp.arange(total_points)[None, :] < point_counts[:, None]).astype(jnp.float32)
    charges = (
        projected * potential(grid_points, charge_sites) * (grid_weights * live)[:, None, :]
    ).astype(jnp.bfloat16)
    spread_back = jnp.einsum(
        "bkp,ks->bps", charges, charge_proj, preferred_element_type=jnp.float32
    ).astype(jnp.bfloat16)
    return jnp.einsum("bfp,bps->bfs", colloc, spread_back, preferred_element_type=jnp.float32)


def on_device(
    occ_coeffs,
    colloc,
    grid_points,
    grid_weights,
    charge_sites,
    charge_proj,
    shell_lists,
    point_counts,
):
    row_count = lax.axis_size("row")
    col_count = lax.axis_size("col")
    owners = row_count * col_count
    me = lax.axis_index("row") * col_count + lax.axis_index("col")
    group_rows = occ_coeffs.shape[0]
    slab_width = charge_proj.shape[1]
    own_rows = group_rows // col_count
    own_blocks = own_rows // SH

    window = broadcast_from_first(occ_coeffs[:slab_width], "row")

    requested = shell_lists.reshape(-1)
    request_count = requested.shape[0]
    capacity = 2 * request_count // owners
    slots = owners * capacity
    owner = requested // own_blocks
    onehot = (owner[:, None] == jnp.arange(owners)[None, :]).astype(jnp.int32)
    before = jnp.cumsum(onehot, axis=0) - onehot
    rank = jnp.sum(before * onehot, axis=1)
    slot = owner * capacity + rank
    hit = slot[None, :] == jnp.arange(slots)[:, None]
    source_of = jnp.sum(jnp.where(hit, jnp.arange(request_count)[None, :], 0), axis=1)
    wanted = jnp.full((slots,), -1, jnp.int32).at[slot].set(requested % own_blocks)
    received_ids = lax.all_to_all(
        wanted.reshape(owners, capacity), ("row", "col"), split_axis=0, concat_axis=0, tiled=True
    ).reshape(-1)

    partial = lax.dot_general(
        occ_coeffs, window, (((1,), (1,)), ((), ())), preferred_element_type=jnp.float32
    )
    pieces = lax.all_to_all(
        partial.reshape(col_count, own_rows, slab_width), "col", split_axis=0, concat_axis=0, tiled=True
    )
    density = jnp.sum(pieces, axis=0).astype(jnp.bfloat16)
    store = density.reshape(own_blocks, SH, slab_width)
    found = store[jnp.maximum(received_ids, 0)]
    replies = lax.all_to_all(
        found.reshape(owners, capacity * SH, slab_width),
        ("row", "col"),
        split_axis=0,
        concat_axis=0,
        tiled=True,
    )
    fetched = replies.reshape(slots, SH, slab_width)[slot]
    dens_rows = fetched.reshape(shell_lists.shape[0], NSIG * SH, slab_width)
    terms = batch_terms(
        dens_rows, colloc, grid_points, grid_weights, charge_sites, charge_proj, point_counts
    )
    terms = terms.astype(jnp.bfloat16).reshape(request_count, SH, slab_width)
    tiles = terms[source_of]
    arrived = lax.all_to_all(
        tiles.reshape(owners, capacity * SH, slab_width),
        ("row", "col"),
        split_axis=0,
        concat_axis=0,
        tiled=True,
    )
    serve = (jnp.arange(own_blocks)[:, None] == received_ids[None, :]).astype(jnp.bfloat16)
    summed = jnp.einsum(
        "js,sfc->jfc", serve, arrived.reshape(slots, SH, slab_width), preferred_element_type=jnp.float32
    )
    return summed.reshape(own_rows, slab_width)


def solution(mesh):
    placed = (
        P("row", "col"),
        P(("row", "col"), None, None),
        P(("row", "col"), None, None),
        P(("row", "col"), None),
        P(),
        P(),
        P(("row", "col"), None),
        P(("row", "col")),
    )
    return jax.shard_map(
        on_device, mesh=mesh, in_specs=placed, out_specs=P(("row", "col"), None), check_vma=False
    )
```

```python
import jax
import jax.numpy as jnp
from jax import lax
from jax.sharding import PartitionSpec as P

SH = 64
NSIG = 16


smear_sq = 0.25


def broadcast_from_first(value, axis):
    size = lax.axis_size(axis)
    index = lax.axis_index(axis)
    if size != 8:
        have = 1
        while have < size:
            pairs = [(src, src + have) for src in range(have) if src + have < size]
            moved = lax.ppermute(value, axis, pairs)
            value = jnp.where(index >= have, moved, value)
            have *= 2
        return value
    first = [lax.ppermute(value, axis, [(0, dst)]) for dst in (1, 2, 6)]
    value = jnp.where(index == 1, first[0], value)
    value = jnp.where(index == 2, first[1], value)
    value = jnp.where(index == 6, first[2], value)
    second = lax.ppermute(value, axis, [(1, 3), (2, 4), (6, 7), (0, 5)])
    return jnp.where((index == 3) | (index == 4) | (index == 5) | (index == 7), second, value)


def potential(points, charge_sites):
    dist_sq = (points[:, 0][:, None, :] - charge_sites[0][None, :, None]) ** 2
    dist_sq = dist_sq + (points[:, 1][:, None, :] - charge_sites[1][None, :, None]) ** 2
    dist_sq = dist_sq + (points[:, 2][:, None, :] - charge_sites[2][None, :, None]) ** 2
    return lax.rsqrt(dist_sq + smear_sq)


def batch_terms(dens_rows, colloc, grid_points, grid_weights, charge_sites, charge_proj, point_counts):
    total_points = colloc.shape[2]
    field = jnp.einsum(
        "bfs,bfp->bsp", dens_rows, colloc, preferred_element_type=jnp.float32
    ).astype(jnp.bfloat16)
    projected = jnp.einsum("ks,bsp->bkp", charge_proj, field, preferred_element_type=jnp.float32)
    live = (jnp.arange(total_points)[None, :] < point_counts[:, None]).astype(jnp.float32)
    charges = (
        projected * potential(grid_points, charge_sites) * (grid_weights * live)[:, None, :]
    ).astype(jnp.bfloat16)
    spread_back = jnp.einsum(
        "bkp,ks->bps", charges, charge_proj, preferred_element_type=jnp.float32
    ).astype(jnp.bfloat16)
    return jnp.einsum("bfp,bps->bfs", colloc, spread_back, preferred_element_type=jnp.float32)


def on_device(
    occ_coeffs,
    colloc,
    grid_points,
    grid_weights,
    charge_sites,
    charge_proj,
    shell_lists,
    point_counts,
):
    row_count = lax.axis_size("row")
    col_count = lax.axis_size("col")
    owners = row_count * col_count
    me = lax.axis_index("row") * col_count + lax.axis_index("col")
    group_rows = occ_coeffs.shape[0]
    slab_width = charge_proj.shape[1]
    own_rows = group_rows // col_count
    own_blocks = own_rows // SH

    window = broadcast_from_first(occ_coeffs[:slab_width], "row")

    requested = shell_lists.reshape(-1)
    request_count = requested.shape[0]
    capacity = 2 * request_count // owners
    slots = owners * capacity
    owner = requested // own_blocks
    onehot = (owner[:, None] == jnp.arange(owners)[None, :]).astype(jnp.int32)
    before = jnp.cumsum(onehot, axis=0) - onehot
    rank = jnp.sum(before * onehot, axis=1)
    slot = owner * capacity + rank
    hit = slot[None, :] == jnp.arange(slots)[:, None]
    source_of = jnp.sum(jnp.where(hit, jnp.arange(request_count)[None, :], 0), axis=1)
    wanted = jnp.full((slots,), -1, jnp.int32).at[slot].set(requested % own_blocks)
    received_ids = lax.all_to_all(
        wanted.reshape(owners, capacity), ("row", "col"), split_axis=0, concat_axis=0, tiled=True
    ).reshape(-1)

    partial = lax.dot_general(
        occ_coeffs, window, (((1,), (1,)), ((), ())), preferred_element_type=jnp.float32
    )
    pieces = lax.all_to_all(
        partial.reshape(col_count, own_rows, slab_width), "col", split_axis=0, concat_axis=0, tiled=True
    )
    density = jnp.sum(pieces, axis=0).astype(jnp.bfloat16)
    store = density.reshape(own_blocks, SH, slab_width)
    found = store[jnp.maximum(received_ids, 0)]
    replies = lax.all_to_all(
        found.reshape(owners, capacity * SH, slab_width),
        ("row", "col"),
        split_axis=0,
        concat_axis=0,
        tiled=True,
    )
    fetched = replies.reshape(slots, SH, slab_width)[slot]
    dens_rows = fetched.reshape(shell_lists.shape[0], NSIG * SH, slab_width)
    terms = batch_terms(
        dens_rows, colloc, grid_points, grid_weights, charge_sites, charge_proj, point_counts
    )
    terms = terms.astype(jnp.bfloat16).reshape(request_count, SH, slab_width)
    tiles = terms[source_of]
    arrived = lax.all_to_all(
        tiles.reshape(owners, capacity * SH, slab_width),
        ("row", "col"),
        split_axis=0,
        concat_axis=0,
        tiled=True,
    )
    serve = (jnp.arange(own_blocks)[:, None] == received_ids[None, :]).astype(jnp.bfloat16)
    summed = jnp.einsum(
        "js,sfc->jfc", serve, arrived.reshape(slots, SH, slab_width), preferred_element_type=jnp.float32
    )
    return summed.reshape(own_rows, slab_width)


def solution(mesh):
    placed = (
        P("row", "col"),
        P(("row", "col"), None, None),
        P(("row", "col"), None, None),
        P(("row", "col"), None),
        P(),
        P(),
        P(("row", "col"), None),
        P(("row", "col")),
    )
    return jax.shard_map(
        on_device, mesh=mesh, in_specs=placed, out_specs=P(("row", "col"), None), check_vma=False
    )
```

```python
import jax
import jax.numpy as jnp
from jax import lax
from jax.sharding import PartitionSpec as P
from jax.experimental import pallas as pl

SH = 64
NSIG = 16


smear_sq = 0.25


def broadcast_from_first(value, axis):
    size = lax.axis_size(axis)
    index = lax.axis_index(axis)
    if size != 8:
        have = 1
        while have < size:
            pairs = [(src, src + have) for src in range(have) if src + have < size]
            moved = lax.ppermute(value, axis, pairs)
            value = jnp.where(index >= have, moved, value)
            have *= 2
        return value
    first = [lax.ppermute(value, axis, [(0, dst)]) for dst in (1, 2, 6)]
    value = jnp.where(index == 1, first[0], value)
    value = jnp.where(index == 2, first[1], value)
    value = jnp.where(index == 6, first[2], value)
    second = lax.ppermute(value, axis, [(1, 3), (2, 4), (6, 7), (0, 5)])
    return jnp.where((index == 3) | (index == 4) | (index == 5) | (index == 7), second, value)


def potential(points, charge_sites):
    dist_sq = (points[:, 0][:, None, :] - charge_sites[0][None, :, None]) ** 2
    dist_sq = dist_sq + (points[:, 1][:, None, :] - charge_sites[1][None, :, None]) ** 2
    dist_sq = dist_sq + (points[:, 2][:, None, :] - charge_sites[2][None, :, None]) ** 2
    return lax.rsqrt(dist_sq + smear_sq)


def batch_kernel(dens_ref, colloc_ref, points_ref, scale_ref, sites_ref, proj_ref, out_ref):
    rows = dens_ref[0]
    values = colloc_ref[0]
    weights = proj_ref[...]
    field = lax.dot_general(
        rows, values, (((0,), (0,)), ((), ())), preferred_element_type=jnp.float32
    ).astype(jnp.bfloat16)
    projected = jnp.dot(weights, field, preferred_element_type=jnp.float32)
    points = points_ref[0]
    sites = sites_ref[...]
    dist_sq = (points[0:1, :] - sites[:, 0:1]) ** 2
    dist_sq = dist_sq + (points[1:2, :] - sites[:, 1:2]) ** 2
    dist_sq = dist_sq + (points[2:3, :] - sites[:, 2:3]) ** 2
    charges = (projected * lax.rsqrt(dist_sq + smear_sq) * scale_ref[0]).astype(jnp.bfloat16)
    spread_back = lax.dot_general(
        weights, charges, (((0,), (0,)), ((), ())), preferred_element_type=jnp.float32
    ).astype(jnp.bfloat16)
    term = lax.dot_general(
        values, spread_back, (((1,), (1,)), ((), ())), preferred_element_type=jnp.float32
    )
    out_ref[0] = term.astype(out_ref.dtype)


def batch_terms(dens_rows, colloc, grid_points, grid_weights, charge_sites, charge_proj, point_counts):
    batches, func_rows, total_points = colloc.shape
    slab_width = charge_proj.shape[1]
    aux = charge_proj.shape[0]
    live = (jnp.arange(total_points)[None, :] < point_counts[:, None]).astype(jnp.float32)
    scale = (grid_weights * live).reshape(batches, 1, total_points)
    sites = jnp.transpose(charge_sites)
    return pl.pallas_call(
        batch_kernel,
        grid=(batches,),
        in_specs=[
            pl.BlockSpec((1, func_rows, slab_width), lambda b: (b, 0, 0)),
            pl.BlockSpec((1, func_rows, total_points), lambda b: (b, 0, 0)),
            pl.BlockSpec((1, 3, total_points), lambda b: (b, 0, 0)),
            pl.BlockSpec((1, 1, total_points), lambda b: (b, 0, 0)),
            pl.BlockSpec((aux, 3), lambda b: (0, 0)),
            pl.BlockSpec((aux, slab_width), lambda b: (0, 0)),
        ],
        out_specs=pl.BlockSpec((1, func_rows, slab_width), lambda b: (b, 0, 0)),
        out_shape=jax.ShapeDtypeStruct((batches, func_rows, slab_width), jnp.bfloat16),
    )(dens_rows, colloc, grid_points, scale, sites, charge_proj)


def on_device(
    occ_coeffs,
    colloc,
    grid_points,
    grid_weights,
    charge_sites,
    charge_proj,
    shell_lists,
    point_counts,
):
    row_count = lax.axis_size("row")
    col_count = lax.axis_size("col")
    owners = row_count * col_count
    me = lax.axis_index("row") * col_count + lax.axis_index("col")
    group_rows = occ_coeffs.shape[0]
    slab_width = charge_proj.shape[1]
    own_rows = group_rows // col_count
    own_blocks = own_rows // SH

    window = broadcast_from_first(occ_coeffs[:slab_width], "row")

    requested = shell_lists.reshape(-1)
    request_count = requested.shape[0]
    capacity = 2 * request_count // owners
    slots = owners * capacity
    owner = requested // own_blocks
    onehot = (owner[:, None] == jnp.arange(owners)[None, :]).astype(jnp.int32)
    before = jnp.cumsum(onehot, axis=0) - onehot
    rank = jnp.sum(before * onehot, axis=1)
    slot = owner * capacity + rank
    hit = slot[None, :] == jnp.arange(slots)[:, None]
    source_of = jnp.sum(jnp.where(hit, jnp.arange(request_count)[None, :], 0), axis=1)
    wanted = jnp.full((slots,), -1, jnp.int32).at[slot].set(requested % own_blocks)
    received_ids = lax.all_to_all(
        wanted.reshape(owners, capacity), ("row", "col"), split_axis=0, concat_axis=0, tiled=True
    ).reshape(-1)

    partial = lax.dot_general(
        occ_coeffs, window, (((1,), (1,)), ((), ())), preferred_element_type=jnp.float32
    )
    pieces = lax.all_to_all(
        partial.reshape(col_count, own_rows, slab_width), "col", split_axis=0, concat_axis=0, tiled=True
    )
    density = jnp.sum(pieces, axis=0).astype(jnp.bfloat16)
    store = density.reshape(own_blocks, SH, slab_width)
    found = store[jnp.maximum(received_ids, 0)]
    replies = lax.all_to_all(
        found.reshape(owners, capacity * SH, slab_width),
        ("row", "col"),
        split_axis=0,
        concat_axis=0,
        tiled=True,
    )
    fetched = replies.reshape(slots, SH, slab_width)[slot]
    dens_rows = fetched.reshape(shell_lists.shape[0], NSIG * SH, slab_width)
    terms = batch_terms(
        dens_rows, colloc, grid_points, grid_weights, charge_sites, charge_proj, point_counts
    )
    terms = terms.reshape(request_count, SH, slab_width)
    tiles = terms[source_of]
    arrived = lax.all_to_all(
        tiles.reshape(owners, capacity * SH, slab_width),
        ("row", "col"),
        split_axis=0,
        concat_axis=0,
        tiled=True,
    )
    serve = (jnp.arange(own_blocks)[:, None] == received_ids[None, :]).astype(jnp.bfloat16)
    summed = jnp.einsum(
        "js,sfc->jfc", serve, arrived.reshape(slots, SH, slab_width), preferred_element_type=jnp.float32
    )
    return summed.reshape(own_rows, slab_width)


def solution(mesh):
    placed = (
        P("row", "col"),
        P(("row", "col"), None, None),
        P(("row", "col"), None, None),
        P(("row", "col"), None),
        P(),
        P(),
        P(("row", "col"), None),
        P(("row", "col")),
    )
    return jax.shard_map(
        on_device, mesh=mesh, in_specs=placed, out_specs=P(("row", "col"), None), check_vma=False
    )
```

```python
import jax
import jax.numpy as jnp
from jax import lax
from jax.sharding import PartitionSpec as P
from jax.experimental import pallas as pl

SH = 64
NSIG = 16


smear_sq = 0.25


def broadcast_from_first(value, axis):
    size = lax.axis_size(axis)
    index = lax.axis_index(axis)
    if size != 8:
        have = 1
        while have < size:
            pairs = [(src, src + have) for src in range(have) if src + have < size]
            moved = lax.ppermute(value, axis, pairs)
            value = jnp.where(index >= have, moved, value)
            have *= 2
        return value
    first = [lax.ppermute(value, axis, [(0, dst)]) for dst in (1, 2, 6)]
    value = jnp.where(index == 1, first[0], value)
    value = jnp.where(index == 2, first[1], value)
    value = jnp.where(index == 6, first[2], value)
    second = lax.ppermute(value, axis, [(1, 3), (2, 4), (6, 7), (0, 5)])
    return jnp.where((index == 3) | (index == 4) | (index == 5) | (index == 7), second, value)


def potential(points, charge_sites):
    dist_sq = (points[:, 0][:, None, :] - charge_sites[0][None, :, None]) ** 2
    dist_sq = dist_sq + (points[:, 1][:, None, :] - charge_sites[1][None, :, None]) ** 2
    dist_sq = dist_sq + (points[:, 2][:, None, :] - charge_sites[2][None, :, None]) ** 2
    return lax.rsqrt(dist_sq + smear_sq)


def batch_kernel(dens_ref, colloc_ref, points_ref, scale_ref, sites_ref, proj_ref, out_ref):
    rows = dens_ref[0]
    values = colloc_ref[0]
    weights = proj_ref[...]
    field = lax.dot_general(
        rows, values, (((0,), (0,)), ((), ())), preferred_element_type=jnp.float32
    ).astype(jnp.bfloat16)
    projected = jnp.dot(weights, field, preferred_element_type=jnp.float32)
    points = points_ref[0]
    sites = sites_ref[...]
    dist_sq = (points[0:1, :] - sites[:, 0:1]) ** 2
    dist_sq = dist_sq + (points[1:2, :] - sites[:, 1:2]) ** 2
    dist_sq = dist_sq + (points[2:3, :] - sites[:, 2:3]) ** 2
    charges = (projected * lax.rsqrt(dist_sq + smear_sq) * scale_ref[0]).astype(jnp.bfloat16)
    spread_back = lax.dot_general(
        weights, charges, (((0,), (0,)), ((), ())), preferred_element_type=jnp.float32
    ).astype(jnp.bfloat16)
    term = lax.dot_general(
        values, spread_back, (((1,), (1,)), ((), ())), preferred_element_type=jnp.float32
    )
    out_ref[0] = term.astype(out_ref.dtype)


def batch_terms(dens_rows, colloc, grid_points, grid_weights, charge_sites, charge_proj, point_counts):
    batches, func_rows, total_points = colloc.shape
    slab_width = charge_proj.shape[1]
    aux = charge_proj.shape[0]
    live = (jnp.arange(total_points)[None, :] < point_counts[:, None]).astype(jnp.float32)
    scale = (grid_weights * live).reshape(batches, 1, total_points)
    sites = jnp.transpose(charge_sites)
    return pl.pallas_call(
        batch_kernel,
        grid=(batches,),
        in_specs=[
            pl.BlockSpec((1, func_rows, slab_width), lambda b: (b, 0, 0)),
            pl.BlockSpec((1, func_rows, total_points), lambda b: (b, 0, 0)),
            pl.BlockSpec((1, 3, total_points), lambda b: (b, 0, 0)),
            pl.BlockSpec((1, 1, total_points), lambda b: (b, 0, 0)),
            pl.BlockSpec((aux, 3), lambda b: (0, 0)),
            pl.BlockSpec((aux, slab_width), lambda b: (0, 0)),
        ],
        out_specs=pl.BlockSpec((1, func_rows, slab_width), lambda b: (b, 0, 0)),
        out_shape=jax.ShapeDtypeStruct((batches, func_rows, slab_width), jnp.bfloat16),
    )(dens_rows, colloc, grid_points, scale, sites, charge_proj)


def product_kernel(coeff_ref, window_ref, out_ref):
    out_ref[...] = lax.dot_general(
        coeff_ref[...], window_ref[...], (((1,), (1,)), ((), ())), preferred_element_type=jnp.float32
    )


def slab_product(occ_coeffs, window):
    rows, depth = occ_coeffs.shape
    width = window.shape[0]
    block = 768 if rows % 768 == 0 else rows
    return pl.pallas_call(
        product_kernel,
        grid=(rows // block,),
        in_specs=[
            pl.BlockSpec((block, depth), lambda i: (i, 0)),
            pl.BlockSpec((width, depth), lambda i: (0, 0)),
        ],
        out_specs=pl.BlockSpec((block, width), lambda i: (i, 0)),
        out_shape=jax.ShapeDtypeStruct((rows, width), jnp.float32),
    )(occ_coeffs, window)


def on_device(
    occ_coeffs,
    colloc,
    grid_points,
    grid_weights,
    charge_sites,
    charge_proj,
    shell_lists,
    point_counts,
):
    row_count = lax.axis_size("row")
    col_count = lax.axis_size("col")
    owners = row_count * col_count
    me = lax.axis_index("row") * col_count + lax.axis_index("col")
    group_rows = occ_coeffs.shape[0]
    slab_width = charge_proj.shape[1]
    own_rows = group_rows // col_count
    own_blocks = own_rows // SH

    window = broadcast_from_first(occ_coeffs[:slab_width], "row")

    requested = shell_lists.reshape(-1)
    request_count = requested.shape[0]
    capacity = 2 * request_count // owners
    slots = owners * capacity
    owner = requested // own_blocks
    onehot = (owner[:, None] == jnp.arange(owners)[None, :]).astype(jnp.int32)
    before = jnp.cumsum(onehot, axis=0) - onehot
    rank = jnp.sum(before * onehot, axis=1)
    slot = owner * capacity + rank
    hit = slot[None, :] == jnp.arange(slots)[:, None]
    source_of = jnp.sum(jnp.where(hit, jnp.arange(request_count)[None, :], 0), axis=1)
    wanted = jnp.full((slots,), -1, jnp.int32).at[slot].set(requested % own_blocks)
    received_ids = lax.all_to_all(
        wanted.reshape(owners, capacity), ("row", "col"), split_axis=0, concat_axis=0, tiled=True
    ).reshape(-1)

    partial = slab_product(occ_coeffs, window)
    pieces = lax.all_to_all(
        partial.reshape(col_count, own_rows, slab_width), "col", split_axis=0, concat_axis=0, tiled=True
    )
    density = jnp.sum(pieces, axis=0).astype(jnp.bfloat16)
    store = density.reshape(own_blocks, SH, slab_width)
    found = store[jnp.maximum(received_ids, 0)]
    replies = lax.all_to_all(
        found.reshape(owners, capacity * SH, slab_width),
        ("row", "col"),
        split_axis=0,
        concat_axis=0,
        tiled=True,
    )
    fetched = replies.reshape(slots, SH, slab_width)[slot]
    dens_rows = fetched.reshape(shell_lists.shape[0], NSIG * SH, slab_width)
    terms = batch_terms(
        dens_rows, colloc, grid_points, grid_weights, charge_sites, charge_proj, point_counts
    )
    terms = terms.reshape(request_count, SH, slab_width)
    tiles = terms[source_of]
    arrived = lax.all_to_all(
        tiles.reshape(owners, capacity * SH, slab_width),
        ("row", "col"),
        split_axis=0,
        concat_axis=0,
        tiled=True,
    )
    serve = (jnp.arange(own_blocks)[:, None] == received_ids[None, :]).astype(jnp.bfloat16)
    summed = jnp.einsum(
        "js,sfc->jfc", serve, arrived.reshape(slots, SH, slab_width), preferred_element_type=jnp.float32
    )
    return summed.reshape(own_rows, slab_width)


def solution(mesh):
    placed = (
        P("row", "col"),
        P(("row", "col"), None, None),
        P(("row", "col"), None, None),
        P(("row", "col"), None),
        P(),
        P(),
        P(("row", "col"), None),
        P(("row", "col")),
    )
    return jax.shard_map(
        on_device, mesh=mesh, in_specs=placed, out_specs=P(("row", "col"), None), check_vma=False
    )
```

```python
import jax
import jax.numpy as jnp
from jax import lax
from jax.sharding import PartitionSpec as P
from jax.experimental import pallas as pl

SH = 64
NSIG = 16


smear_sq = 0.25


def broadcast_from_first(value, axis):
    size = lax.axis_size(axis)
    index = lax.axis_index(axis)
    if size != 8:
        have = 1
        while have < size:
            pairs = [(src, src + have) for src in range(have) if src + have < size]
            moved = lax.ppermute(value, axis, pairs)
            value = jnp.where(index >= have, moved, value)
            have *= 2
        return value
    first = [lax.ppermute(value, axis, [(0, dst)]) for dst in (1, 2, 6)]
    value = jnp.where(index == 1, first[0], value)
    value = jnp.where(index == 2, first[1], value)
    value = jnp.where(index == 6, first[2], value)
    second = lax.ppermute(value, axis, [(1, 3), (2, 4), (6, 7), (0, 5)])
    return jnp.where((index == 3) | (index == 4) | (index == 5) | (index == 7), second, value)


def potential(points, charge_sites):
    dist_sq = (points[:, 0][:, None, :] - charge_sites[0][None, :, None]) ** 2
    dist_sq = dist_sq + (points[:, 1][:, None, :] - charge_sites[1][None, :, None]) ** 2
    dist_sq = dist_sq + (points[:, 2][:, None, :] - charge_sites[2][None, :, None]) ** 2
    return lax.rsqrt(dist_sq + smear_sq)


def batch_kernel(dens_ref, colloc_ref, points_ref, scale_ref, sites_ref, proj_ref, out_ref):
    rows = dens_ref[0]
    values = colloc_ref[0]
    weights = proj_ref[...]
    field = lax.dot_general(
        rows, values, (((0,), (0,)), ((), ())), preferred_element_type=jnp.float32
    ).astype(jnp.bfloat16)
    projected = jnp.dot(weights, field, preferred_element_type=jnp.float32)
    points = points_ref[0]
    sites = sites_ref[...]
    dist_sq = (points[0:1, :] - sites[:, 0:1]) ** 2
    dist_sq = dist_sq + (points[1:2, :] - sites[:, 1:2]) ** 2
    dist_sq = dist_sq + (points[2:3, :] - sites[:, 2:3]) ** 2
    charges = (projected * lax.rsqrt(dist_sq + smear_sq) * scale_ref[0]).astype(jnp.bfloat16)
    spread_back = lax.dot_general(
        weights, charges, (((0,), (0,)), ((), ())), preferred_element_type=jnp.float32
    ).astype(jnp.bfloat16)
    term = lax.dot_general(
        values, spread_back, (((1,), (1,)), ((), ())), preferred_element_type=jnp.float32
    )
    out_ref[0] = term.astype(out_ref.dtype)


def batch_terms(dens_rows, colloc, grid_points, grid_weights, charge_sites, charge_proj, point_counts):
    batches, func_rows, total_points = colloc.shape
    slab_width = charge_proj.shape[1]
    aux = charge_proj.shape[0]
    live = (jnp.arange(total_points)[None, :] < point_counts[:, None]).astype(jnp.float32)
    scale = (grid_weights * live).reshape(batches, 1, total_points)
    sites = jnp.transpose(charge_sites)
    return pl.pallas_call(
        batch_kernel,
        grid=(batches,),
        in_specs=[
            pl.BlockSpec((1, func_rows, slab_width), lambda b: (b, 0, 0)),
            pl.BlockSpec((1, func_rows, total_points), lambda b: (b, 0, 0)),
            pl.BlockSpec((1, 3, total_points), lambda b: (b, 0, 0)),
            pl.BlockSpec((1, 1, total_points), lambda b: (b, 0, 0)),
            pl.BlockSpec((aux, 3), lambda b: (0, 0)),
            pl.BlockSpec((aux, slab_width), lambda b: (0, 0)),
        ],
        out_specs=pl.BlockSpec((1, func_rows, slab_width), lambda b: (b, 0, 0)),
        out_shape=jax.ShapeDtypeStruct((batches, func_rows, slab_width), jnp.bfloat16),
    )(dens_rows, colloc, grid_points, scale, sites, charge_proj)


def product_kernel(coeff_ref, window_ref, out_ref):
    out_ref[...] = jnp.dot(coeff_ref[...], window_ref[...], preferred_element_type=jnp.float32)


def slab_product(occ_coeffs, window):
    rows, depth = occ_coeffs.shape
    width = window.shape[0]
    block = 1536 if rows % 1536 == 0 else rows
    return pl.pallas_call(
        product_kernel,
        grid=(rows // block,),
        in_specs=[
            pl.BlockSpec((block, depth), lambda i: (i, 0)),
            pl.BlockSpec((depth, width), lambda i: (0, 0)),
        ],
        out_specs=pl.BlockSpec((block, width), lambda i: (i, 0)),
        out_shape=jax.ShapeDtypeStruct((rows, width), jnp.float32),
    )(occ_coeffs, jnp.transpose(window))


def on_device(
    occ_coeffs,
    colloc,
    grid_points,
    grid_weights,
    charge_sites,
    charge_proj,
    shell_lists,
    point_counts,
):
    row_count = lax.axis_size("row")
    col_count = lax.axis_size("col")
    owners = row_count * col_count
    me = lax.axis_index("row") * col_count + lax.axis_index("col")
    group_rows = occ_coeffs.shape[0]
    slab_width = charge_proj.shape[1]
    own_rows = group_rows // col_count
    own_blocks = own_rows // SH

    window = broadcast_from_first(occ_coeffs[:slab_width], "row")

    requested = shell_lists.reshape(-1)
    request_count = requested.shape[0]
    capacity = 2 * request_count // owners
    slots = owners * capacity
    owner = requested // own_blocks
    onehot = (owner[:, None] == jnp.arange(owners)[None, :]).astype(jnp.int32)
    before = jnp.cumsum(onehot, axis=0) - onehot
    rank = jnp.sum(before * onehot, axis=1)
    slot = owner * capacity + rank
    hit = slot[None, :] == jnp.arange(slots)[:, None]
    source_of = jnp.sum(jnp.where(hit, jnp.arange(request_count)[None, :], 0), axis=1)
    wanted = jnp.full((slots,), -1, jnp.int32).at[slot].set(requested % own_blocks)
    received_ids = lax.all_to_all(
        wanted.reshape(owners, capacity), ("row", "col"), split_axis=0, concat_axis=0, tiled=True
    ).reshape(-1)

    partial = slab_product(occ_coeffs, window)
    pieces = lax.all_to_all(
        partial.reshape(col_count, own_rows, slab_width), "col", split_axis=0, concat_axis=0, tiled=True
    )
    density = jnp.sum(pieces, axis=0).astype(jnp.bfloat16)
    store = density.reshape(own_blocks, SH, slab_width)
    found = store[jnp.maximum(received_ids, 0)]
    replies = lax.all_to_all(
        found.reshape(owners, capacity * SH, slab_width),
        ("row", "col"),
        split_axis=0,
        concat_axis=0,
        tiled=True,
    )
    fetched = replies.reshape(slots, SH, slab_width)[slot]
    dens_rows = fetched.reshape(shell_lists.shape[0], NSIG * SH, slab_width)
    terms = batch_terms(
        dens_rows, colloc, grid_points, grid_weights, charge_sites, charge_proj, point_counts
    )
    terms = terms.reshape(request_count, SH, slab_width)
    tiles = terms[source_of]
    arrived = lax.all_to_all(
        tiles.reshape(owners, capacity * SH, slab_width),
        ("row", "col"),
        split_axis=0,
        concat_axis=0,
        tiled=True,
    )
    serve = (jnp.arange(own_blocks)[:, None] == received_ids[None, :]).astype(jnp.bfloat16)
    summed = jnp.einsum(
        "js,sfc->jfc", serve, arrived.reshape(slots, SH, slab_width), preferred_element_type=jnp.float32
    )
    return summed.reshape(own_rows, slab_width)


def solution(mesh):
    placed = (
        P("row", "col"),
        P(("row", "col"), None, None),
        P(("row", "col"), None, None),
        P(("row", "col"), None),
        P(),
        P(),
        P(("row", "col"), None),
        P(("row", "col")),
    )
    return jax.shard_map(
        on_device, mesh=mesh, in_specs=placed, out_specs=P(("row", "col"), None), check_vma=False
    )
```

```python
import jax
import jax.numpy as jnp
from jax import lax
from jax.sharding import PartitionSpec as P
from jax.experimental import pallas as pl
from jax.experimental.pallas import tpu as pltpu

SH = 64
NSIG = 16


smear_sq = 0.25


def broadcast_from_first(value, axis):
    size = lax.axis_size(axis)
    index = lax.axis_index(axis)
    if size != 8:
        have = 1
        while have < size:
            pairs = [(src, src + have) for src in range(have) if src + have < size]
            moved = lax.ppermute(value, axis, pairs)
            value = jnp.where(index >= have, moved, value)
            have *= 2
        return value
    first = [lax.ppermute(value, axis, [(0, dst)]) for dst in (1, 2, 6)]
    value = jnp.where(index == 1, first[0], value)
    value = jnp.where(index == 2, first[1], value)
    value = jnp.where(index == 6, first[2], value)
    second = lax.ppermute(value, axis, [(1, 3), (2, 4), (6, 7), (0, 5)])
    return jnp.where((index == 3) | (index == 4) | (index == 5) | (index == 7), second, value)


def potential(points, charge_sites):
    dist_sq = (points[:, 0][:, None, :] - charge_sites[0][None, :, None]) ** 2
    dist_sq = dist_sq + (points[:, 1][:, None, :] - charge_sites[1][None, :, None]) ** 2
    dist_sq = dist_sq + (points[:, 2][:, None, :] - charge_sites[2][None, :, None]) ** 2
    return lax.rsqrt(dist_sq + smear_sq)


def batch_kernel(slot_ref, *refs):
    blocks = refs[:NSIG]
    colloc_ref, points_ref, scale_ref, sites_ref, proj_ref, _, out_ref, rows_ref, term_ref, sems = refs[NSIG:]
    b = pl.program_id(0)
    for k in range(NSIG):
        rows_ref[k * SH:(k + 1) * SH, :] = blocks[k][0]
    values = colloc_ref[0]
    weights = proj_ref[...]
    field = lax.dot_general(
        rows_ref[...], values, (((0,), (0,)), ((), ())), preferred_element_type=jnp.float32
    ).astype(jnp.bfloat16)
    projected = jnp.dot(weights, field, preferred_element_type=jnp.float32)
    points = points_ref[0]
    sites = sites_ref[...]
    dist_sq = (points[0:1, :] - sites[:, 0:1]) ** 2
    dist_sq = dist_sq + (points[1:2, :] - sites[:, 1:2]) ** 2
    dist_sq = dist_sq + (points[2:3, :] - sites[:, 2:3]) ** 2
    charges = (projected * lax.rsqrt(dist_sq + smear_sq) * scale_ref[0]).astype(jnp.bfloat16)
    spread_back = lax.dot_general(
        weights, charges, (((0,), (0,)), ((), ())), preferred_element_type=jnp.float32
    ).astype(jnp.bfloat16)
    term = lax.dot_general(
        values, spread_back, (((1,), (1,)), ((), ())), preferred_element_type=jnp.float32
    )
    term_ref[...] = term.astype(term_ref.dtype)
    copies = []
    for k in range(NSIG):
        copy = pltpu.make_async_copy(
            term_ref.at[pl.ds(k * SH, SH)], out_ref.at[slot_ref[b * NSIG + k]], sems.at[k]
        )
        copy.start()
        copies.append(copy)
    for copy in copies:
        copy.wait()


def batch_terms(replies, slot, colloc, grid_points, grid_weights, charge_sites, charge_proj, point_counts):
    batches, func_rows, total_points = colloc.shape
    slots = replies.shape[0]
    slab_width = charge_proj.shape[1]
    aux = charge_proj.shape[0]
    live = (jnp.arange(total_points)[None, :] < point_counts[:, None]).astype(jnp.float32)
    scale = (grid_weights * live).reshape(batches, 1, total_points)
    sites = jnp.transpose(charge_sites)

    def block_spec(k):
        return pl.BlockSpec((1, SH, slab_width), lambda b, slot_ref: (slot_ref[b * NSIG + k], 0, 0))

    grid_spec = pltpu.PrefetchScalarGridSpec(
        num_scalar_prefetch=1,
        grid=(batches,),
        in_specs=[block_spec(k) for k in range(NSIG)]
        + [
            pl.BlockSpec((1, func_rows, total_points), lambda b, slot_ref: (b, 0, 0)),
            pl.BlockSpec((1, 3, total_points), lambda b, slot_ref: (b, 0, 0)),
            pl.BlockSpec((1, 1, total_points), lambda b, slot_ref: (b, 0, 0)),
            pl.BlockSpec((aux, 3), lambda b, slot_ref: (0, 0)),
            pl.BlockSpec((aux, slab_width), lambda b, slot_ref: (0, 0)),
            pl.BlockSpec(memory_space=pl.ANY),
        ],
        out_specs=pl.BlockSpec(memory_space=pl.ANY),
        scratch_shapes=[
            pltpu.VMEM((func_rows, slab_width), jnp.bfloat16),
            pltpu.VMEM((func_rows, slab_width), jnp.bfloat16),
            pltpu.SemaphoreType.DMA((NSIG,)),
        ],
    )
    empty = jnp.zeros((slots, SH, slab_width), jnp.bfloat16)
    return pl.pallas_call(
        batch_kernel,
        grid_spec=grid_spec,
        out_shape=jax.ShapeDtypeStruct((slots, SH, slab_width), jnp.bfloat16),
        input_output_aliases={1 + NSIG + 5: 0},
    )(slot, *([replies] * NSIG), colloc, grid_points, scale, sites, charge_proj, empty)


def product_kernel(coeff_ref, window_ref, out_ref):
    out_ref[...] = jnp.dot(coeff_ref[...], window_ref[...], preferred_element_type=jnp.float32)


def slab_product(occ_coeffs, window):
    rows, depth = occ_coeffs.shape
    width = window.shape[0]
    block = 1536 if rows % 1536 == 0 else rows
    return pl.pallas_call(
        product_kernel,
        grid=(rows // block,),
        in_specs=[
            pl.BlockSpec((block, depth), lambda i: (i, 0)),
            pl.BlockSpec((depth, width), lambda i: (0, 0)),
        ],
        out_specs=pl.BlockSpec((block, width), lambda i: (i, 0)),
        out_shape=jax.ShapeDtypeStruct((rows, width), jnp.float32),
    )(occ_coeffs, jnp.transpose(window))


def on_device(
    occ_coeffs,
    colloc,
    grid_points,
    grid_weights,
    charge_sites,
    charge_proj,
    shell_lists,
    point_counts,
):
    row_count = lax.axis_size("row")
    col_count = lax.axis_size("col")
    owners = row_count * col_count
    me = lax.axis_index("row") * col_count + lax.axis_index("col")
    group_rows = occ_coeffs.shape[0]
    slab_width = charge_proj.shape[1]
    own_rows = group_rows // col_count
    own_blocks = own_rows // SH

    window = broadcast_from_first(occ_coeffs[:slab_width], "row")

    requested = shell_lists.reshape(-1)
    request_count = requested.shape[0]
    capacity = 2 * request_count // owners
    slots = owners * capacity
    owner = requested // own_blocks
    onehot = (owner[:, None] == jnp.arange(owners)[None, :]).astype(jnp.int32)
    before = jnp.cumsum(onehot, axis=0) - onehot
    rank = jnp.sum(before * onehot, axis=1)
    slot = owner * capacity + rank
    hit = slot[None, :] == jnp.arange(slots)[:, None]
    source_of = jnp.sum(jnp.where(hit, jnp.arange(request_count)[None, :], 0), axis=1)
    wanted = jnp.full((slots,), -1, jnp.int32).at[slot].set(requested % own_blocks)
    received_ids = lax.all_to_all(
        wanted.reshape(owners, capacity), ("row", "col"), split_axis=0, concat_axis=0, tiled=True
    ).reshape(-1)

    partial = slab_product(occ_coeffs, window)
    pieces = lax.all_to_all(
        partial.reshape(col_count, own_rows, slab_width), "col", split_axis=0, concat_axis=0, tiled=True
    )
    density = jnp.sum(pieces, axis=0).astype(jnp.bfloat16)
    store = density.reshape(own_blocks, SH, slab_width)
    found = store[jnp.maximum(received_ids, 0)]
    replies = lax.all_to_all(
        found.reshape(owners, capacity * SH, slab_width),
        ("row", "col"),
        split_axis=0,
        concat_axis=0,
        tiled=True,
    )
    tiles = batch_terms(
        replies.reshape(slots, SH, slab_width),
        jnp.clip(slot, 0, slots - 1),
        colloc,
        grid_points,
        grid_weights,
        charge_sites,
        charge_proj,
        point_counts,
    )
    arrived = lax.all_to_all(
        tiles.reshape(owners, capacity * SH, slab_width),
        ("row", "col"),
        split_axis=0,
        concat_axis=0,
        tiled=True,
    )
    serve = (jnp.arange(own_blocks)[:, None] == received_ids[None, :]).astype(jnp.bfloat16)
    summed = jnp.einsum(
        "js,sfc->jfc", serve, arrived.reshape(slots, SH, slab_width), preferred_element_type=jnp.float32
    )
    return summed.reshape(own_rows, slab_width)


def solution(mesh):
    placed = (
        P("row", "col"),
        P(("row", "col"), None, None),
        P(("row", "col"), None, None),
        P(("row", "col"), None),
        P(),
        P(),
        P(("row", "col"), None),
        P(("row", "col")),
    )
    return jax.shard_map(
        on_device, mesh=mesh, in_specs=placed, out_specs=P(("row", "col"), None), check_vma=False
    )
```

```python
import jax
import jax.numpy as jnp
from jax import lax
from jax.sharding import PartitionSpec as P
from jax.experimental import pallas as pl
from jax.experimental.pallas import tpu as pltpu

SH = 64
NSIG = 16


smear_sq = 0.25


def broadcast_from_first(value, axis):
    size = lax.axis_size(axis)
    index = lax.axis_index(axis)
    if size != 8:
        have = 1
        while have < size:
            pairs = [(src, src + have) for src in range(have) if src + have < size]
            moved = lax.ppermute(value, axis, pairs)
            value = jnp.where(index >= have, moved, value)
            have *= 2
        return value
    first = [lax.ppermute(value, axis, [(0, dst)]) for dst in (1, 2, 6)]
    value = jnp.where(index == 1, first[0], value)
    value = jnp.where(index == 2, first[1], value)
    value = jnp.where(index == 6, first[2], value)
    second = lax.ppermute(value, axis, [(1, 3), (2, 4), (6, 7), (0, 5)])
    return jnp.where((index == 3) | (index == 4) | (index == 5) | (index == 7), second, value)


def potential(points, charge_sites):
    dist_sq = (points[:, 0][:, None, :] - charge_sites[0][None, :, None]) ** 2
    dist_sq = dist_sq + (points[:, 1][:, None, :] - charge_sites[1][None, :, None]) ** 2
    dist_sq = dist_sq + (points[:, 2][:, None, :] - charge_sites[2][None, :, None]) ** 2
    return lax.rsqrt(dist_sq + smear_sq)


def batch_kernel(slot_ref, *refs):
    blocks = refs[:NSIG]
    colloc_ref, points_ref, scale_ref, sites_ref, proj_ref, out_ref, rows_ref = refs[NSIG:]
    for k in range(NSIG):
        rows_ref[k * SH:(k + 1) * SH, :] = blocks[k][0]
    values = colloc_ref[0]
    weights = proj_ref[...]
    field = lax.dot_general(
        rows_ref[...], values, (((0,), (0,)), ((), ())), preferred_element_type=jnp.float32
    ).astype(jnp.bfloat16)
    projected = jnp.dot(weights, field, preferred_element_type=jnp.float32)
    points = points_ref[0]
    sites = sites_ref[...]
    dist_sq = (points[0:1, :] - sites[:, 0:1]) ** 2
    dist_sq = dist_sq + (points[1:2, :] - sites[:, 1:2]) ** 2
    dist_sq = dist_sq + (points[2:3, :] - sites[:, 2:3]) ** 2
    charges = (projected * lax.rsqrt(dist_sq + smear_sq) * scale_ref[0]).astype(jnp.bfloat16)
    spread_back = lax.dot_general(
        weights, charges, (((0,), (0,)), ((), ())), preferred_element_type=jnp.float32
    ).astype(jnp.bfloat16)
    term = lax.dot_general(
        values, spread_back, (((1,), (1,)), ((), ())), preferred_element_type=jnp.float32
    )
    out_ref[0] = term.astype(out_ref.dtype)


def batch_terms(replies, slot, colloc, grid_points, grid_weights, charge_sites, charge_proj, point_counts):
    batches, func_rows, total_points = colloc.shape
    slab_width = charge_proj.shape[1]
    aux = charge_proj.shape[0]
    live = (jnp.arange(total_points)[None, :] < point_counts[:, None]).astype(jnp.float32)
    scale = (grid_weights * live).reshape(batches, 1, total_points)
    sites = jnp.transpose(charge_sites)

    def block_spec(k):
        return pl.BlockSpec((1, SH, slab_width), lambda b, slot_ref: (slot_ref[b * NSIG + k], 0, 0))

    grid_spec = pltpu.PrefetchScalarGridSpec(
        num_scalar_prefetch=1,
        grid=(batches,),
        in_specs=[block_spec(k) for k in range(NSIG)]
        + [
            pl.BlockSpec((1, func_rows, total_points), lambda b, slot_ref: (b, 0, 0)),
            pl.BlockSpec((1, 3, total_points), lambda b, slot_ref: (b, 0, 0)),
            pl.BlockSpec((1, 1, total_points), lambda b, slot_ref: (b, 0, 0)),
            pl.BlockSpec((aux, 3), lambda b, slot_ref: (0, 0)),
            pl.BlockSpec((aux, slab_width), lambda b, slot_ref: (0, 0)),
        ],
        out_specs=pl.BlockSpec((1, func_rows, slab_width), lambda b, slot_ref: (b, 0, 0)),
        scratch_shapes=[pltpu.VMEM((func_rows, slab_width), jnp.bfloat16)],
    )
    return pl.pallas_call(
        batch_kernel,
        grid_spec=grid_spec,
        out_shape=jax.ShapeDtypeStruct((batches, func_rows, slab_width), jnp.bfloat16),
    )(slot, *([replies] * NSIG), colloc, grid_points, scale, sites, charge_proj)


def product_kernel(coeff_ref, window_ref, out_ref):
    out_ref[...] = jnp.dot(coeff_ref[...], window_ref[...], preferred_element_type=jnp.float32)


def slab_product(occ_coeffs, window):
    rows, depth = occ_coeffs.shape
    width = window.shape[0]
    block = 1536 if rows % 1536 == 0 else rows
    return pl.pallas_call(
        product_kernel,
        grid=(rows // block,),
        in_specs=[
            pl.BlockSpec((block, depth), lambda i: (i, 0)),
            pl.BlockSpec((depth, width), lambda i: (0, 0)),
        ],
        out_specs=pl.BlockSpec((block, width), lambda i: (i, 0)),
        out_shape=jax.ShapeDtypeStruct((rows, width), jnp.float32),
    )(occ_coeffs, jnp.transpose(window))


def on_device(
    occ_coeffs,
    colloc,
    grid_points,
    grid_weights,
    charge_sites,
    charge_proj,
    shell_lists,
    point_counts,
):
    row_count = lax.axis_size("row")
    col_count = lax.axis_size("col")
    owners = row_count * col_count
    me = lax.axis_index("row") * col_count + lax.axis_index("col")
    group_rows = occ_coeffs.shape[0]
    slab_width = charge_proj.shape[1]
    own_rows = group_rows // col_count
    own_blocks = own_rows // SH

    window = broadcast_from_first(occ_coeffs[:slab_width], "row")

    requested = shell_lists.reshape(-1)
    request_count = requested.shape[0]
    capacity = 2 * request_count // owners
    slots = owners * capacity
    owner = requested // own_blocks
    onehot = (owner[:, None] == jnp.arange(owners)[None, :]).astype(jnp.int32)
    before = jnp.cumsum(onehot, axis=0) - onehot
    rank = jnp.sum(before * onehot, axis=1)
    slot = owner * capacity + rank
    hit = slot[None, :] == jnp.arange(slots)[:, None]
    source_of = jnp.sum(jnp.where(hit, jnp.arange(request_count)[None, :], 0), axis=1)
    wanted = jnp.full((slots,), -1, jnp.int32).at[slot].set(requested % own_blocks)
    received_ids = lax.all_to_all(
        wanted.reshape(owners, capacity), ("row", "col"), split_axis=0, concat_axis=0, tiled=True
    ).reshape(-1)

    partial = slab_product(occ_coeffs, window)
    pieces = lax.all_to_all(
        partial.reshape(col_count, own_rows, slab_width), "col", split_axis=0, concat_axis=0, tiled=True
    )
    density = jnp.sum(pieces, axis=0).astype(jnp.bfloat16)
    store = density.reshape(own_blocks, SH, slab_width)
    found = store[jnp.maximum(received_ids, 0)]
    replies = lax.all_to_all(
        found.reshape(owners, capacity * SH, slab_width),
        ("row", "col"),
        split_axis=0,
        concat_axis=0,
        tiled=True,
    )
    terms = batch_terms(
        replies.reshape(slots, SH, slab_width),
        jnp.clip(slot, 0, slots - 1),
        colloc,
        grid_points,
        grid_weights,
        charge_sites,
        charge_proj,
        point_counts,
    )
    tiles = terms.reshape(request_count, SH, slab_width)[source_of]
    arrived = lax.all_to_all(
        tiles.reshape(owners, capacity * SH, slab_width),
        ("row", "col"),
        split_axis=0,
        concat_axis=0,
        tiled=True,
    )
    serve = (jnp.arange(own_blocks)[:, None] == received_ids[None, :]).astype(jnp.bfloat16)
    summed = jnp.einsum(
        "js,sfc->jfc", serve, arrived.reshape(slots, SH, slab_width), preferred_element_type=jnp.float32
    )
    return summed.reshape(own_rows, slab_width)


def solution(mesh):
    placed = (
        P("row", "col"),
        P(("row", "col"), None, None),
        P(("row", "col"), None, None),
        P(("row", "col"), None),
        P(),
        P(),
        P(("row", "col"), None),
        P(("row", "col")),
    )
    return jax.shard_map(
        on_device, mesh=mesh, in_specs=placed, out_specs=P(("row", "col"), None), check_vma=False
    )
```

```python
import jax
import jax.numpy as jnp
from jax import lax
from jax.sharding import PartitionSpec as P
from jax.experimental import pallas as pl
from jax.experimental.pallas import tpu as pltpu

SH = 64
NSIG = 16


smear_sq = 0.25


def broadcast_from_first(value, axis):
    size = lax.axis_size(axis)
    index = lax.axis_index(axis)
    if size != 8:
        have = 1
        while have < size:
            pairs = [(src, src + have) for src in range(have) if src + have < size]
            moved = lax.ppermute(value, axis, pairs)
            value = jnp.where(index >= have, moved, value)
            have *= 2
        return value
    for dst in range(1, size):
        moved = lax.ppermute(value, axis, [(0, dst)])
        value = jnp.where(index == dst, moved, value)
    return value


def potential(points, charge_sites):
    dist_sq = (points[:, 0][:, None, :] - charge_sites[0][None, :, None]) ** 2
    dist_sq = dist_sq + (points[:, 1][:, None, :] - charge_sites[1][None, :, None]) ** 2
    dist_sq = dist_sq + (points[:, 2][:, None, :] - charge_sites[2][None, :, None]) ** 2
    return lax.rsqrt(dist_sq + smear_sq)


def batch_kernel(slot_ref, *refs):
    blocks = refs[:NSIG]
    colloc_ref, points_ref, scale_ref, sites_ref, proj_ref, out_ref, rows_ref = refs[NSIG:]
    for k in range(NSIG):
        rows_ref[k * SH:(k + 1) * SH, :] = blocks[k][0]
    values = colloc_ref[0]
    weights = proj_ref[...]
    field = lax.dot_general(
        rows_ref[...], values, (((0,), (0,)), ((), ())), preferred_element_type=jnp.float32
    ).astype(jnp.bfloat16)
    projected = jnp.dot(weights, field, preferred_element_type=jnp.float32)
    points = points_ref[0]
    sites = sites_ref[...]
    dist_sq = (points[0:1, :] - sites[:, 0:1]) ** 2
    dist_sq = dist_sq + (points[1:2, :] - sites[:, 1:2]) ** 2
    dist_sq = dist_sq + (points[2:3, :] - sites[:, 2:3]) ** 2
    charges = (projected * lax.rsqrt(dist_sq + smear_sq) * scale_ref[0]).astype(jnp.bfloat16)
    spread_back = lax.dot_general(
        weights, charges, (((0,), (0,)), ((), ())), preferred_element_type=jnp.float32
    ).astype(jnp.bfloat16)
    term = lax.dot_general(
        values, spread_back, (((1,), (1,)), ((), ())), preferred_element_type=jnp.float32
    )
    out_ref[0] = term.astype(out_ref.dtype)


def batch_terms(replies, slot, colloc, grid_points, grid_weights, charge_sites, charge_proj, point_counts):
    batches, func_rows, total_points = colloc.shape
    slab_width = charge_proj.shape[1]
    aux = charge_proj.shape[0]
    live = (jnp.arange(total_points)[None, :] < point_counts[:, None]).astype(jnp.float32)
    scale = (grid_weights * live).reshape(batches, 1, total_points)
    sites = jnp.transpose(charge_sites)

    def block_spec(k):
        return pl.BlockSpec((1, SH, slab_width), lambda b, slot_ref: (slot_ref[b * NSIG + k], 0, 0))

    grid_spec = pltpu.PrefetchScalarGridSpec(
        num_scalar_prefetch=1,
        grid=(batches,),
        in_specs=[block_spec(k) for k in range(NSIG)]
        + [
            pl.BlockSpec((1, func_rows, total_points), lambda b, slot_ref: (b, 0, 0)),
            pl.BlockSpec((1, 3, total_points), lambda b, slot_ref: (b, 0, 0)),
            pl.BlockSpec((1, 1, total_points), lambda b, slot_ref: (b, 0, 0)),
            pl.BlockSpec((aux, 3), lambda b, slot_ref: (0, 0)),
            pl.BlockSpec((aux, slab_width), lambda b, slot_ref: (0, 0)),
        ],
        out_specs=pl.BlockSpec((1, func_rows, slab_width), lambda b, slot_ref: (b, 0, 0)),
        scratch_shapes=[pltpu.VMEM((func_rows, slab_width), jnp.bfloat16)],
    )
    return pl.pallas_call(
        batch_kernel,
        grid_spec=grid_spec,
        out_shape=jax.ShapeDtypeStruct((batches, func_rows, slab_width), jnp.bfloat16),
    )(slot, *([replies] * NSIG), colloc, grid_points, scale, sites, charge_proj)


def product_kernel(coeff_ref, window_ref, out_ref):
    out_ref[...] = jnp.dot(coeff_ref[...], window_ref[...], preferred_element_type=jnp.float32)


def slab_product(occ_coeffs, window):
    rows, depth = occ_coeffs.shape
    width = window.shape[0]
    block = 1536 if rows % 1536 == 0 else rows
    return pl.pallas_call(
        product_kernel,
        grid=(rows // block,),
        in_specs=[
            pl.BlockSpec((block, depth), lambda i: (i, 0)),
            pl.BlockSpec((depth, width), lambda i: (0, 0)),
        ],
        out_specs=pl.BlockSpec((block, width), lambda i: (i, 0)),
        out_shape=jax.ShapeDtypeStruct((rows, width), jnp.float32),
    )(occ_coeffs, jnp.transpose(window))


def on_device(
    occ_coeffs,
    colloc,
    grid_points,
    grid_weights,
    charge_sites,
    charge_proj,
    shell_lists,
    point_counts,
):
    row_count = lax.axis_size("row")
    col_count = lax.axis_size("col")
    owners = row_count * col_count
    me = lax.axis_index("row") * col_count + lax.axis_index("col")
    group_rows = occ_coeffs.shape[0]
    slab_width = charge_proj.shape[1]
    own_rows = group_rows // col_count
    own_blocks = own_rows // SH

    window = broadcast_from_first(occ_coeffs[:slab_width], "row")

    requested = shell_lists.reshape(-1)
    request_count = requested.shape[0]
    capacity = 2 * request_count // owners
    slots = owners * capacity
    owner = requested // own_blocks
    onehot = (owner[:, None] == jnp.arange(owners)[None, :]).astype(jnp.int32)
    before = jnp.cumsum(onehot, axis=0) - onehot
    rank = jnp.sum(before * onehot, axis=1)
    slot = owner * capacity + rank
    hit = slot[None, :] == jnp.arange(slots)[:, None]
    source_of = jnp.sum(jnp.where(hit, jnp.arange(request_count)[None, :], 0), axis=1)
    wanted = jnp.full((slots,), -1, jnp.int32).at[slot].set(requested % own_blocks)
    received_ids = lax.all_to_all(
        wanted.reshape(owners, capacity), ("row", "col"), split_axis=0, concat_axis=0, tiled=True
    ).reshape(-1)

    partial = slab_product(occ_coeffs, window)
    pieces = lax.all_to_all(
        partial.reshape(col_count, own_rows, slab_width), "col", split_axis=0, concat_axis=0, tiled=True
    )
    density = jnp.sum(pieces, axis=0).astype(jnp.bfloat16)
    store = density.reshape(own_blocks, SH, slab_width)
    found = store[jnp.maximum(received_ids, 0)]
    replies = lax.all_to_all(
        found.reshape(owners, capacity * SH, slab_width),
        ("row", "col"),
        split_axis=0,
        concat_axis=0,
        tiled=True,
    )
    terms = batch_terms(
        replies.reshape(slots, SH, slab_width),
        jnp.clip(slot, 0, slots - 1),
        colloc,
        grid_points,
        grid_weights,
        charge_sites,
        charge_proj,
        point_counts,
    )
    tiles = terms.reshape(request_count, SH, slab_width)[source_of]
    arrived = lax.all_to_all(
        tiles.reshape(owners, capacity * SH, slab_width),
        ("row", "col"),
        split_axis=0,
        concat_axis=0,
        tiled=True,
    )
    serve = (jnp.arange(own_blocks)[:, None] == received_ids[None, :]).astype(jnp.bfloat16)
    summed = jnp.einsum(
        "js,sfc->jfc", serve, arrived.reshape(slots, SH, slab_width), preferred_element_type=jnp.float32
    )
    return summed.reshape(own_rows, slab_width)


def solution(mesh):
    placed = (
        P("row", "col"),
        P(("row", "col"), None, None),
        P(("row", "col"), None, None),
        P(("row", "col"), None),
        P(),
        P(),
        P(("row", "col"), None),
        P(("row", "col")),
    )
    return jax.shard_map(
        on_device, mesh=mesh, in_specs=placed, out_specs=P(("row", "col"), None), check_vma=False
    )
```

```python
import jax
import jax.numpy as jnp
from jax import lax
from jax.sharding import PartitionSpec as P
from jax.experimental import pallas as pl
from jax.experimental.pallas import tpu as pltpu

SH = 64
NSIG = 16


smear_sq = 0.25


def broadcast_from_first(value, axis):
    size = lax.axis_size(axis)
    index = lax.axis_index(axis)
    if size != 8:
        have = 1
        while have < size:
            pairs = [(src, src + have) for src in range(have) if src + have < size]
            moved = lax.ppermute(value, axis, pairs)
            value = jnp.where(index >= have, moved, value)
            have *= 2
        return value
    first = [lax.ppermute(value, axis, [(0, dst)]) for dst in (1, 2, 6)]
    value = jnp.where(index == 1, first[0], value)
    value = jnp.where(index == 2, first[1], value)
    value = jnp.where(index == 6, first[2], value)
    second = lax.ppermute(value, axis, [(1, 3), (2, 4), (6, 7), (0, 5)])
    return jnp.where((index == 3) | (index == 4) | (index == 5) | (index == 7), second, value)


def potential(points, charge_sites):
    dist_sq = (points[:, 0][:, None, :] - charge_sites[0][None, :, None]) ** 2
    dist_sq = dist_sq + (points[:, 1][:, None, :] - charge_sites[1][None, :, None]) ** 2
    dist_sq = dist_sq + (points[:, 2][:, None, :] - charge_sites[2][None, :, None]) ** 2
    return lax.rsqrt(dist_sq + smear_sq)


def batch_kernel(slot_ref, *refs):
    blocks = refs[:NSIG]
    colloc_ref, points_ref, scale_ref, sites_ref, proj_ref, out_ref, rows_ref = refs[NSIG:]
    for k in range(NSIG):
        rows_ref[k * SH:(k + 1) * SH, :] = blocks[k][0]
    values = colloc_ref[0]
    weights = proj_ref[...]
    field = lax.dot_general(
        rows_ref[...], values, (((0,), (0,)), ((), ())), preferred_element_type=jnp.float32
    ).astype(jnp.bfloat16)
    projected = jnp.dot(weights, field, preferred_element_type=jnp.float32)
    points = points_ref[0]
    sites = sites_ref[...]
    dist_sq = (points[0:1, :] - sites[:, 0:1]) ** 2
    dist_sq = dist_sq + (points[1:2, :] - sites[:, 1:2]) ** 2
    dist_sq = dist_sq + (points[2:3, :] - sites[:, 2:3]) ** 2
    charges = (projected * lax.rsqrt(dist_sq + smear_sq) * scale_ref[0]).astype(jnp.bfloat16)
    spread_back = lax.dot_general(
        weights, charges, (((0,), (0,)), ((), ())), preferred_element_type=jnp.float32
    ).astype(jnp.bfloat16)
    term = lax.dot_general(
        values, spread_back, (((1,), (1,)), ((), ())), preferred_element_type=jnp.float32
    )
    out_ref[0] = term.astype(out_ref.dtype)


def batch_terms(replies, slot, colloc, grid_points, grid_weights, charge_sites, charge_proj, point_counts):
    batches, func_rows, total_points = colloc.shape
    slab_width = charge_proj.shape[1]
    aux = charge_proj.shape[0]
    live = (jnp.arange(total_points)[None, :] < point_counts[:, None]).astype(jnp.float32)
    scale = (grid_weights * live).reshape(batches, 1, total_points)
    sites = jnp.transpose(charge_sites)

    def block_spec(k):
        return pl.BlockSpec((1, SH, slab_width), lambda b, slot_ref: (slot_ref[b * NSIG + k], 0, 0))

    grid_spec = pltpu.PrefetchScalarGridSpec(
        num_scalar_prefetch=1,
        grid=(batches,),
        in_specs=[block_spec(k) for k in range(NSIG)]
        + [
            pl.BlockSpec((1, func_rows, total_points), lambda b, slot_ref: (b, 0, 0)),
            pl.BlockSpec((1, 3, total_points), lambda b, slot_ref: (b, 0, 0)),
            pl.BlockSpec((1, 1, total_points), lambda b, slot_ref: (b, 0, 0)),
            pl.BlockSpec((aux, 3), lambda b, slot_ref: (0, 0)),
            pl.BlockSpec((aux, slab_width), lambda b, slot_ref: (0, 0)),
        ],
        out_specs=pl.BlockSpec((1, func_rows, slab_width), lambda b, slot_ref: (b, 0, 0)),
        scratch_shapes=[pltpu.VMEM((func_rows, slab_width), jnp.bfloat16)],
    )
    return pl.pallas_call(
        batch_kernel,
        grid_spec=grid_spec,
        out_shape=jax.ShapeDtypeStruct((batches, func_rows, slab_width), jnp.bfloat16),
    )(slot, *([replies] * NSIG), colloc, grid_points, scale, sites, charge_proj)


def product_kernel(coeff_ref, window_ref, out_ref):
    out_ref[...] = jnp.dot(coeff_ref[...], window_ref[...], preferred_element_type=jnp.float32)


def slab_product(occ_coeffs, window):
    rows, depth = occ_coeffs.shape
    width = window.shape[0]
    block = 768 if rows % 768 == 0 else rows
    return pl.pallas_call(
        product_kernel,
        grid=(rows // block,),
        in_specs=[
            pl.BlockSpec((block, depth), lambda i: (i, 0)),
            pl.BlockSpec((depth, width), lambda i: (0, 0)),
        ],
        out_specs=pl.BlockSpec((block, width), lambda i: (i, 0)),
        out_shape=jax.ShapeDtypeStruct((rows, width), jnp.float32),
    )(occ_coeffs, jnp.transpose(window))


def on_device(
    occ_coeffs,
    colloc,
    grid_points,
    grid_weights,
    charge_sites,
    charge_proj,
    shell_lists,
    point_counts,
):
    row_count = lax.axis_size("row")
    col_count = lax.axis_size("col")
    owners = row_count * col_count
    me = lax.axis_index("row") * col_count + lax.axis_index("col")
    group_rows = occ_coeffs.shape[0]
    slab_width = charge_proj.shape[1]
    own_rows = group_rows // col_count
    own_blocks = own_rows // SH

    window = broadcast_from_first(occ_coeffs[:slab_width], "row")

    requested = shell_lists.reshape(-1)
    request_count = requested.shape[0]
    capacity = 2 * request_count // owners
    slots = owners * capacity
    owner = requested // own_blocks
    onehot = (owner[:, None] == jnp.arange(owners)[None, :]).astype(jnp.int32)
    before = jnp.cumsum(onehot, axis=0) - onehot
    rank = jnp.sum(before * onehot, axis=1)
    slot = owner * capacity + rank
    hit = slot[None, :] == jnp.arange(slots)[:, None]
    source_of = jnp.sum(jnp.where(hit, jnp.arange(request_count)[None, :], 0), axis=1)
    wanted = jnp.full((slots,), -1, jnp.int32).at[slot].set(requested % own_blocks)
    received_ids = lax.all_to_all(
        wanted.reshape(owners, capacity), ("row", "col"), split_axis=0, concat_axis=0, tiled=True
    ).reshape(-1)

    partial = slab_product(occ_coeffs, window)
    pieces = lax.all_to_all(
        partial.reshape(col_count, own_rows, slab_width), "col", split_axis=0, concat_axis=0, tiled=True
    )
    density = jnp.sum(pieces, axis=0).astype(jnp.bfloat16)
    store = density.reshape(own_blocks, SH, slab_width)
    found = store[jnp.maximum(received_ids, 0)]
    replies = lax.all_to_all(
        found.reshape(owners, capacity * SH, slab_width),
        ("row", "col"),
        split_axis=0,
        concat_axis=0,
        tiled=True,
    )
    terms = batch_terms(
        replies.reshape(slots, SH, slab_width),
        jnp.clip(slot, 0, slots - 1),
        colloc,
        grid_points,
        grid_weights,
        charge_sites,
        charge_proj,
        point_counts,
    )
    tiles = terms.reshape(request_count, SH, slab_width)[source_of]
    arrived = lax.all_to_all(
        tiles.reshape(owners, capacity * SH, slab_width),
        ("row", "col"),
        split_axis=0,
        concat_axis=0,
        tiled=True,
    )
    serve = (jnp.arange(own_blocks)[:, None] == received_ids[None, :]).astype(jnp.bfloat16)
    summed = jnp.einsum(
        "js,sfc->jfc", serve, arrived.reshape(slots, SH, slab_width), preferred_element_type=jnp.float32
    )
    return summed.reshape(own_rows, slab_width)


def solution(mesh):
    placed = (
        P("row", "col"),
        P(("row", "col"), None, None),
        P(("row", "col"), None, None),
        P(("row", "col"), None),
        P(),
        P(),
        P(("row", "col"), None),
        P(("row", "col")),
    )
    return jax.shard_map(
        on_device, mesh=mesh, in_specs=placed, out_specs=P(("row", "col"), None), check_vma=False
    )
```

```python
import jax
import jax.numpy as jnp
from jax import lax
from jax.sharding import PartitionSpec as P
from jax.experimental import pallas as pl
from jax.experimental.pallas import tpu as pltpu

SH = 64
NSIG = 16


smear_sq = 0.25


def broadcast_from_first(value, axis):
    size = lax.axis_size(axis)
    index = lax.axis_index(axis)
    if size != 8:
        have = 1
        while have < size:
            pairs = [(src, src + have) for src in range(have) if src + have < size]
            moved = lax.ppermute(value, axis, pairs)
            value = jnp.where(index >= have, moved, value)
            have *= 2
        return value
    first = [lax.ppermute(value, axis, [(0, dst)]) for dst in (1, 2, 6)]
    value = jnp.where(index == 1, first[0], value)
    value = jnp.where(index == 2, first[1], value)
    value = jnp.where(index == 6, first[2], value)
    second = lax.ppermute(value, axis, [(1, 3), (2, 4), (6, 7), (0, 5)])
    return jnp.where((index == 3) | (index == 4) | (index == 5) | (index == 7), second, value)


def potential(points, charge_sites):
    dist_sq = (points[:, 0][:, None, :] - charge_sites[0][None, :, None]) ** 2
    dist_sq = dist_sq + (points[:, 1][:, None, :] - charge_sites[1][None, :, None]) ** 2
    dist_sq = dist_sq + (points[:, 2][:, None, :] - charge_sites[2][None, :, None]) ** 2
    return lax.rsqrt(dist_sq + smear_sq)


def batch_kernel(slot_ref, *refs):
    blocks = refs[:NSIG]
    colloc_ref, points_ref, scale_ref, sites_ref, proj_ref, out_ref, rows_ref = refs[NSIG:]
    for k in range(NSIG):
        rows_ref[k * SH:(k + 1) * SH, :] = blocks[k][0]
    values = colloc_ref[0]
    weights = proj_ref[...]
    field = lax.dot_general(
        rows_ref[...], values, (((0,), (0,)), ((), ())), preferred_element_type=jnp.float32
    ).astype(jnp.bfloat16)
    projected = jnp.dot(weights, field, preferred_element_type=jnp.float32)
    points = points_ref[0]
    sites = sites_ref[...]
    dist_sq = (points[0:1, :] - sites[:, 0:1]) ** 2
    dist_sq = dist_sq + (points[1:2, :] - sites[:, 1:2]) ** 2
    dist_sq = dist_sq + (points[2:3, :] - sites[:, 2:3]) ** 2
    charges = (projected * lax.rsqrt(dist_sq + smear_sq) * scale_ref[0]).astype(jnp.bfloat16)
    spread_back = lax.dot_general(
        weights, charges, (((0,), (0,)), ((), ())), preferred_element_type=jnp.float32
    ).astype(jnp.bfloat16)
    term = lax.dot_general(
        values, spread_back, (((1,), (1,)), ((), ())), preferred_element_type=jnp.float32
    )
    out_ref[0] = term.astype(out_ref.dtype)


def batch_terms(replies, slot, colloc, grid_points, grid_weights, charge_sites, charge_proj, point_counts):
    batches, func_rows, total_points = colloc.shape
    slab_width = charge_proj.shape[1]
    aux = charge_proj.shape[0]
    live = (jnp.arange(total_points)[None, :] < point_counts[:, None]).astype(jnp.float32)
    scale = (grid_weights * live).reshape(batches, 1, total_points)
    sites = jnp.transpose(charge_sites)

    def block_spec(k):
        return pl.BlockSpec((1, SH, slab_width), lambda b, slot_ref: (slot_ref[b * NSIG + k], 0, 0))

    grid_spec = pltpu.PrefetchScalarGridSpec(
        num_scalar_prefetch=1,
        grid=(batches,),
        in_specs=[block_spec(k) for k in range(NSIG)]
        + [
            pl.BlockSpec((1, func_rows, total_points), lambda b, slot_ref: (b, 0, 0)),
            pl.BlockSpec((1, 3, total_points), lambda b, slot_ref: (b, 0, 0)),
            pl.BlockSpec((1, 1, total_points), lambda b, slot_ref: (b, 0, 0)),
            pl.BlockSpec((aux, 3), lambda b, slot_ref: (0, 0)),
            pl.BlockSpec((aux, slab_width), lambda b, slot_ref: (0, 0)),
        ],
        out_specs=pl.BlockSpec((1, func_rows, slab_width), lambda b, slot_ref: (b, 0, 0)),
        scratch_shapes=[pltpu.VMEM((func_rows, slab_width), jnp.bfloat16)],
    )
    return pl.pallas_call(
        batch_kernel,
        grid_spec=grid_spec,
        out_shape=jax.ShapeDtypeStruct((batches, func_rows, slab_width), jnp.bfloat16),
    )(slot, *([replies] * NSIG), colloc, grid_points, scale, sites, charge_proj)


def product_kernel(coeff_ref, window_ref, out_ref):
    out_ref[...] = jnp.dot(coeff_ref[...], window_ref[...], preferred_element_type=jnp.float32)


def slab_product(occ_coeffs, window):
    rows, depth = occ_coeffs.shape
    width = window.shape[0]
    block = 3072 if rows % 3072 == 0 else rows
    return pl.pallas_call(
        product_kernel,
        grid=(rows // block,),
        in_specs=[
            pl.BlockSpec((block, depth), lambda i: (i, 0)),
            pl.BlockSpec((depth, width), lambda i: (0, 0)),
        ],
        out_specs=pl.BlockSpec((block, width), lambda i: (i, 0)),
        out_shape=jax.ShapeDtypeStruct((rows, width), jnp.float32),
    )(occ_coeffs, jnp.transpose(window))


def on_device(
    occ_coeffs,
    colloc,
    grid_points,
    grid_weights,
    charge_sites,
    charge_proj,
    shell_lists,
    point_counts,
):
    row_count = lax.axis_size("row")
    col_count = lax.axis_size("col")
    owners = row_count * col_count
    me = lax.axis_index("row") * col_count + lax.axis_index("col")
    group_rows = occ_coeffs.shape[0]
    slab_width = charge_proj.shape[1]
    own_rows = group_rows // col_count
    own_blocks = own_rows // SH

    window = broadcast_from_first(occ_coeffs[:slab_width], "row")

    requested = shell_lists.reshape(-1)
    request_count = requested.shape[0]
    capacity = 2 * request_count // owners
    slots = owners * capacity
    owner = requested // own_blocks
    onehot = (owner[:, None] == jnp.arange(owners)[None, :]).astype(jnp.int32)
    before = jnp.cumsum(onehot, axis=0) - onehot
    rank = jnp.sum(before * onehot, axis=1)
    slot = owner * capacity + rank
    hit = slot[None, :] == jnp.arange(slots)[:, None]
    source_of = jnp.sum(jnp.where(hit, jnp.arange(request_count)[None, :], 0), axis=1)
    wanted = jnp.full((slots,), -1, jnp.int32).at[slot].set(requested % own_blocks)
    received_ids = lax.all_to_all(
        wanted.reshape(owners, capacity), ("row", "col"), split_axis=0, concat_axis=0, tiled=True
    ).reshape(-1)

    partial = slab_product(occ_coeffs, window)
    pieces = lax.all_to_all(
        partial.reshape(col_count, own_rows, slab_width), "col", split_axis=0, concat_axis=0, tiled=True
    )
    density = jnp.sum(pieces, axis=0).astype(jnp.bfloat16)
    store = density.reshape(own_blocks, SH, slab_width)
    found = store[jnp.maximum(received_ids, 0)]
    replies = lax.all_to_all(
        found.reshape(owners, capacity * SH, slab_width),
        ("row", "col"),
        split_axis=0,
        concat_axis=0,
        tiled=True,
    )
    terms = batch_terms(
        replies.reshape(slots, SH, slab_width),
        jnp.clip(slot, 0, slots - 1),
        colloc,
        grid_points,
        grid_weights,
        charge_sites,
        charge_proj,
        point_counts,
    )
    tiles = terms.reshape(request_count, SH, slab_width)[source_of]
    arrived = lax.all_to_all(
        tiles.reshape(owners, capacity * SH, slab_width),
        ("row", "col"),
        split_axis=0,
        concat_axis=0,
        tiled=True,
    )
    serve = (jnp.arange(own_blocks)[:, None] == received_ids[None, :]).astype(jnp.bfloat16)
    summed = jnp.einsum(
        "js,sfc->jfc", serve, arrived.reshape(slots, SH, slab_width), preferred_element_type=jnp.float32
    )
    return summed.reshape(own_rows, slab_width)


def solution(mesh):
    placed = (
        P("row", "col"),
        P(("row", "col"), None, None),
        P(("row", "col"), None, None),
        P(("row", "col"), None),
        P(),
        P(),
        P(("row", "col"), None),
        P(("row", "col")),
    )
    return jax.shard_map(
        on_device, mesh=mesh, in_specs=placed, out_specs=P(("row", "col"), None), check_vma=False
    )
```

```python
import jax
import jax.numpy as jnp
from jax import lax
from jax.sharding import PartitionSpec as P
from jax.experimental import pallas as pl
from jax.experimental.pallas import tpu as pltpu

SH = 64
NSIG = 16


smear_sq = 0.25


def broadcast_from_first(value, axis):
    size = lax.axis_size(axis)
    index = lax.axis_index(axis)
    if size != 8:
        have = 1
        while have < size:
            pairs = [(src, src + have) for src in range(have) if src + have < size]
            moved = lax.ppermute(value, axis, pairs)
            value = jnp.where(index >= have, moved, value)
            have *= 2
        return value
    first = [lax.ppermute(value, axis, [(0, dst)]) for dst in (1, 2, 6)]
    value = jnp.where(index == 1, first[0], value)
    value = jnp.where(index == 2, first[1], value)
    value = jnp.where(index == 6, first[2], value)
    second = lax.ppermute(value, axis, [(1, 3), (2, 4), (6, 7), (0, 5)])
    return jnp.where((index == 3) | (index == 4) | (index == 5) | (index == 7), second, value)


def potential(points, charge_sites):
    dist_sq = (points[:, 0][:, None, :] - charge_sites[0][None, :, None]) ** 2
    dist_sq = dist_sq + (points[:, 1][:, None, :] - charge_sites[1][None, :, None]) ** 2
    dist_sq = dist_sq + (points[:, 2][:, None, :] - charge_sites[2][None, :, None]) ** 2
    return lax.rsqrt(dist_sq + smear_sq)


def batch_kernel(slot_ref, *refs):
    per_step = (len(refs) - 7) // NSIG
    blocks = refs[:NSIG * per_step]
    colloc_ref, points_ref, scale_ref, sites_ref, proj_ref, out_ref, rows_ref = refs[NSIG * per_step:]
    weights = proj_ref[...]
    sites = sites_ref[...]
    for t in range(per_step):
        for k in range(NSIG):
            rows_ref[k * SH:(k + 1) * SH, :] = blocks[t * NSIG + k][0]
        values = colloc_ref[t]
        field = lax.dot_general(
            rows_ref[...], values, (((0,), (0,)), ((), ())), preferred_element_type=jnp.float32
        ).astype(jnp.bfloat16)
        projected = jnp.dot(weights, field, preferred_element_type=jnp.float32)
        points = points_ref[t]
        dist_sq = (points[0:1, :] - sites[:, 0:1]) ** 2
        dist_sq = dist_sq + (points[1:2, :] - sites[:, 1:2]) ** 2
        dist_sq = dist_sq + (points[2:3, :] - sites[:, 2:3]) ** 2
        charges = (projected * lax.rsqrt(dist_sq + smear_sq) * scale_ref[t]).astype(jnp.bfloat16)
        spread_back = lax.dot_general(
            weights, charges, (((0,), (0,)), ((), ())), preferred_element_type=jnp.float32
        ).astype(jnp.bfloat16)
        term = lax.dot_general(
            values, spread_back, (((1,), (1,)), ((), ())), preferred_element_type=jnp.float32
        )
        out_ref[t] = term.astype(out_ref.dtype)


def batch_terms(replies, slot, colloc, grid_points, grid_weights, charge_sites, charge_proj, point_counts):
    batches, func_rows, total_points = colloc.shape
    slab_width = charge_proj.shape[1]
    aux = charge_proj.shape[0]
    live = (jnp.arange(total_points)[None, :] < point_counts[:, None]).astype(jnp.float32)
    scale = (grid_weights * live).reshape(batches, 1, total_points)
    sites = jnp.transpose(charge_sites)

    per_step = 2 if batches % 2 == 0 else 1

    def block_spec(i):
        return pl.BlockSpec(
            (1, SH, slab_width), lambda b, slot_ref: (slot_ref[b * per_step * NSIG + i], 0, 0)
        )

    grid_spec = pltpu.PrefetchScalarGridSpec(
        num_scalar_prefetch=1,
        grid=(batches // per_step,),
        in_specs=[block_spec(i) for i in range(NSIG * per_step)]
        + [
            pl.BlockSpec((per_step, func_rows, total_points), lambda b, slot_ref: (b, 0, 0)),
            pl.BlockSpec((per_step, 3, total_points), lambda b, slot_ref: (b, 0, 0)),
            pl.BlockSpec((per_step, 1, total_points), lambda b, slot_ref: (b, 0, 0)),
            pl.BlockSpec((aux, 3), lambda b, slot_ref: (0, 0)),
            pl.BlockSpec((aux, slab_width), lambda b, slot_ref: (0, 0)),
        ],
        out_specs=pl.BlockSpec((per_step, func_rows, slab_width), lambda b, slot_ref: (b, 0, 0)),
        scratch_shapes=[pltpu.VMEM((func_rows, slab_width), jnp.bfloat16)],
    )
    return pl.pallas_call(
        batch_kernel,
        grid_spec=grid_spec,
        out_shape=jax.ShapeDtypeStruct((batches, func_rows, slab_width), jnp.bfloat16),
    )(slot, *([replies] * (NSIG * per_step)), colloc, grid_points, scale, sites, charge_proj)


def product_kernel(coeff_ref, window_ref, out_ref):
    out_ref[...] = jnp.dot(coeff_ref[...], window_ref[...], preferred_element_type=jnp.float32)


def slab_product(occ_coeffs, window):
    rows, depth = occ_coeffs.shape
    width = window.shape[0]
    block = 3072 if rows % 3072 == 0 else rows
    return pl.pallas_call(
        product_kernel,
        grid=(rows // block,),
        in_specs=[
            pl.BlockSpec((block, depth), lambda i: (i, 0)),
            pl.BlockSpec((depth, width), lambda i: (0, 0)),
        ],
        out_specs=pl.BlockSpec((block, width), lambda i: (i, 0)),
        out_shape=jax.ShapeDtypeStruct((rows, width), jnp.float32),
    )(occ_coeffs, jnp.transpose(window))


def on_device(
    occ_coeffs,
    colloc,
    grid_points,
    grid_weights,
    charge_sites,
    charge_proj,
    shell_lists,
    point_counts,
):
    row_count = lax.axis_size("row")
    col_count = lax.axis_size("col")
    owners = row_count * col_count
    me = lax.axis_index("row") * col_count + lax.axis_index("col")
    group_rows = occ_coeffs.shape[0]
    slab_width = charge_proj.shape[1]
    own_rows = group_rows // col_count
    own_blocks = own_rows // SH

    window = broadcast_from_first(occ_coeffs[:slab_width], "row")

    requested = shell_lists.reshape(-1)
    request_count = requested.shape[0]
    capacity = 2 * request_count // owners
    slots = owners * capacity
    owner = requested // own_blocks
    onehot = (owner[:, None] == jnp.arange(owners)[None, :]).astype(jnp.int32)
    before = jnp.cumsum(onehot, axis=0) - onehot
    rank = jnp.sum(before * onehot, axis=1)
    slot = owner * capacity + rank
    hit = slot[None, :] == jnp.arange(slots)[:, None]
    source_of = jnp.sum(jnp.where(hit, jnp.arange(request_count)[None, :], 0), axis=1)
    wanted = jnp.full((slots,), -1, jnp.int32).at[slot].set(requested % own_blocks)
    received_ids = lax.all_to_all(
        wanted.reshape(owners, capacity), ("row", "col"), split_axis=0, concat_axis=0, tiled=True
    ).reshape(-1)

    partial = slab_product(occ_coeffs, window)
    pieces = lax.all_to_all(
        partial.reshape(col_count, own_rows, slab_width), "col", split_axis=0, concat_axis=0, tiled=True
    )
    density = jnp.sum(pieces, axis=0).astype(jnp.bfloat16)
    store = density.reshape(own_blocks, SH, slab_width)
    found = store[jnp.maximum(received_ids, 0)]
    replies = lax.all_to_all(
        found.reshape(owners, capacity * SH, slab_width),
        ("row", "col"),
        split_axis=0,
        concat_axis=0,
        tiled=True,
    )
    terms = batch_terms(
        replies.reshape(slots, SH, slab_width),
        jnp.clip(slot, 0, slots - 1),
        colloc,
        grid_points,
        grid_weights,
        charge_sites,
        charge_proj,
        point_counts,
    )
    tiles = terms.reshape(request_count, SH, slab_width)[source_of]
    arrived = lax.all_to_all(
        tiles.reshape(owners, capacity * SH, slab_width),
        ("row", "col"),
        split_axis=0,
        concat_axis=0,
        tiled=True,
    )
    serve = (jnp.arange(own_blocks)[:, None] == received_ids[None, :]).astype(jnp.bfloat16)
    summed = jnp.einsum(
        "js,sfc->jfc", serve, arrived.reshape(slots, SH, slab_width), preferred_element_type=jnp.float32
    )
    return summed.reshape(own_rows, slab_width)


def solution(mesh):
    placed = (
        P("row", "col"),
        P(("row", "col"), None, None),
        P(("row", "col"), None, None),
        P(("row", "col"), None),
        P(),
        P(),
        P(("row", "col"), None),
        P(("row", "col")),
    )
    return jax.shard_map(
        on_device, mesh=mesh, in_specs=placed, out_specs=P(("row", "col"), None), check_vma=False
    )
```

```python
import jax
import jax.numpy as jnp
from jax import lax
from jax.sharding import PartitionSpec as P
from jax.experimental import pallas as pl
from jax.experimental.pallas import tpu as pltpu

SH = 64
NSIG = 16


smear_sq = 0.25


def broadcast_from_first(value, axis):
    size = lax.axis_size(axis)
    index = lax.axis_index(axis)
    if size != 8:
        have = 1
        while have < size:
            pairs = [(src, src + have) for src in range(have) if src + have < size]
            moved = lax.ppermute(value, axis, pairs)
            value = jnp.where(index >= have, moved, value)
            have *= 2
        return value
    first = [lax.ppermute(value, axis, [(0, dst)]) for dst in (1, 2, 6)]
    value = jnp.where(index == 1, first[0], value)
    value = jnp.where(index == 2, first[1], value)
    value = jnp.where(index == 6, first[2], value)
    second = lax.ppermute(value, axis, [(1, 3), (2, 4), (6, 7), (0, 5)])
    return jnp.where((index == 3) | (index == 4) | (index == 5) | (index == 7), second, value)


def potential(points, charge_sites):
    dist_sq = (points[:, 0][:, None, :] - charge_sites[0][None, :, None]) ** 2
    dist_sq = dist_sq + (points[:, 1][:, None, :] - charge_sites[1][None, :, None]) ** 2
    dist_sq = dist_sq + (points[:, 2][:, None, :] - charge_sites[2][None, :, None]) ** 2
    return lax.rsqrt(dist_sq + smear_sq)


def batch_kernel(slot_ref, *refs):
    blocks = refs[:NSIG]
    colloc_ref, points_ref, scale_ref, sites_ref, proj_ref, out_ref, rows_ref = refs[NSIG:]
    for k in range(NSIG):
        rows_ref[k * SH:(k + 1) * SH, :] = blocks[k][0]
    values = colloc_ref[0]
    weights = proj_ref[...]
    field = lax.dot_general(
        rows_ref[...], values, (((0,), (0,)), ((), ())), preferred_element_type=jnp.float32
    ).astype(jnp.bfloat16)
    projected = jnp.dot(weights, field, preferred_element_type=jnp.float32)
    points = points_ref[0]
    sites = sites_ref[...]
    dist_sq = (points[0:1, :] - sites[:, 0:1]) ** 2
    dist_sq = dist_sq + (points[1:2, :] - sites[:, 1:2]) ** 2
    dist_sq = dist_sq + (points[2:3, :] - sites[:, 2:3]) ** 2
    charges = (projected * lax.rsqrt(dist_sq + smear_sq) * scale_ref[0]).astype(jnp.bfloat16)
    spread_back = lax.dot_general(
        weights, charges, (((0,), (0,)), ((), ())), preferred_element_type=jnp.float32
    ).astype(jnp.bfloat16)
    term = lax.dot_general(
        values, spread_back, (((1,), (1,)), ((), ())), preferred_element_type=jnp.float32
    )
    out_ref[0] = term.astype(out_ref.dtype)


def batch_terms(replies, slot, colloc, grid_points, grid_weights, charge_sites, charge_proj, point_counts):
    batches, func_rows, total_points = colloc.shape
    slab_width = charge_proj.shape[1]
    aux = charge_proj.shape[0]
    live = (jnp.arange(total_points)[None, :] < point_counts[:, None]).astype(jnp.float32)
    scale = (grid_weights * live).reshape(batches, 1, total_points)
    sites = jnp.transpose(charge_sites)

    def block_spec(k):
        return pl.BlockSpec((1, SH, slab_width), lambda b, slot_ref: (slot_ref[b * NSIG + k], 0, 0))

    grid_spec = pltpu.PrefetchScalarGridSpec(
        num_scalar_prefetch=1,
        grid=(batches,),
        in_specs=[block_spec(k) for k in range(NSIG)]
        + [
            pl.BlockSpec((1, func_rows, total_points), lambda b, slot_ref: (b, 0, 0)),
            pl.BlockSpec((1, 3, total_points), lambda b, slot_ref: (b, 0, 0)),
            pl.BlockSpec((1, 1, total_points), lambda b, slot_ref: (b, 0, 0)),
            pl.BlockSpec((aux, 3), lambda b, slot_ref: (0, 0)),
            pl.BlockSpec((aux, slab_width), lambda b, slot_ref: (0, 0)),
        ],
        out_specs=pl.BlockSpec((1, func_rows, slab_width), lambda b, slot_ref: (b, 0, 0)),
        scratch_shapes=[pltpu.VMEM((func_rows, slab_width), jnp.bfloat16)],
    )
    return pl.pallas_call(
        batch_kernel,
        grid_spec=grid_spec,
        out_shape=jax.ShapeDtypeStruct((batches, func_rows, slab_width), jnp.bfloat16),
    )(slot, *([replies] * NSIG), colloc, grid_points, scale, sites, charge_proj)


def product_kernel(coeff_ref, window_ref, out_ref):
    out_ref[...] = jnp.dot(coeff_ref[...], window_ref[...], preferred_element_type=jnp.float32)


def slab_product(occ_coeffs, window):
    rows, depth = occ_coeffs.shape
    width = window.shape[0]
    block = 2048 if rows % 2048 == 0 else rows
    return pl.pallas_call(
        product_kernel,
        grid=(rows // block,),
        in_specs=[
            pl.BlockSpec((block, depth), lambda i: (i, 0)),
            pl.BlockSpec((depth, width), lambda i: (0, 0)),
        ],
        out_specs=pl.BlockSpec((block, width), lambda i: (i, 0)),
        out_shape=jax.ShapeDtypeStruct((rows, width), jnp.float32),
    )(occ_coeffs, jnp.transpose(window))


def on_device(
    occ_coeffs,
    colloc,
    grid_points,
    grid_weights,
    charge_sites,
    charge_proj,
    shell_lists,
    point_counts,
):
    row_count = lax.axis_size("row")
    col_count = lax.axis_size("col")
    owners = row_count * col_count
    me = lax.axis_index("row") * col_count + lax.axis_index("col")
    group_rows = occ_coeffs.shape[0]
    slab_width = charge_proj.shape[1]
    own_rows = group_rows // col_count
    own_blocks = own_rows // SH

    window = broadcast_from_first(occ_coeffs[:slab_width], "row")

    requested = shell_lists.reshape(-1)
    request_count = requested.shape[0]
    capacity = 2 * request_count // owners
    slots = owners * capacity
    owner = requested // own_blocks
    onehot = (owner[:, None] == jnp.arange(owners)[None, :]).astype(jnp.int32)
    before = jnp.cumsum(onehot, axis=0) - onehot
    rank = jnp.sum(before * onehot, axis=1)
    slot = owner * capacity + rank
    hit = slot[None, :] == jnp.arange(slots)[:, None]
    source_of = jnp.sum(jnp.where(hit, jnp.arange(request_count)[None, :], 0), axis=1)
    wanted = jnp.full((slots,), -1, jnp.int32).at[slot].set(requested % own_blocks)
    received_ids = lax.all_to_all(
        wanted.reshape(owners, capacity), ("row", "col"), split_axis=0, concat_axis=0, tiled=True
    ).reshape(-1)

    partial = slab_product(occ_coeffs, window)
    pieces = lax.all_to_all(
        partial.reshape(col_count, own_rows, slab_width), "col", split_axis=0, concat_axis=0, tiled=True
    )
    density = jnp.sum(pieces, axis=0).astype(jnp.bfloat16)
    store = density.reshape(own_blocks, SH, slab_width)
    found = store[jnp.maximum(received_ids, 0)]
    replies = lax.all_to_all(
        found.reshape(owners, capacity * SH, slab_width),
        ("row", "col"),
        split_axis=0,
        concat_axis=0,
        tiled=True,
    )
    terms = batch_terms(
        replies.reshape(slots, SH, slab_width),
        jnp.clip(slot, 0, slots - 1),
        colloc,
        grid_points,
        grid_weights,
        charge_sites,
        charge_proj,
        point_counts,
    )
    tiles = terms.reshape(request_count, SH, slab_width)[source_of]
    arrived = lax.all_to_all(
        tiles.reshape(owners, capacity * SH, slab_width),
        ("row", "col"),
        split_axis=0,
        concat_axis=0,
        tiled=True,
    )
    serve = (jnp.arange(own_blocks)[:, None] == received_ids[None, :]).astype(jnp.bfloat16)
    summed = jnp.einsum(
        "js,sfc->jfc", serve, arrived.reshape(slots, SH, slab_width), preferred_element_type=jnp.float32
    )
    return summed.reshape(own_rows, slab_width)


def solution(mesh):
    placed = (
        P("row", "col"),
        P(("row", "col"), None, None),
        P(("row", "col"), None, None),
        P(("row", "col"), None),
        P(),
        P(),
        P(("row", "col"), None),
        P(("row", "col")),
    )
    return jax.shard_map(
        on_device, mesh=mesh, in_specs=placed, out_specs=P(("row", "col"), None), check_vma=False
    )
```
